768 devices in a mesh: dp: 128 (over y, x, z_lo), pipe: 6 (over z_hi, core).
Axes of the slice: x: 4, y: 8, z: 12 (z_hi: 3, z_lo: 4; z = z_hi * 4 + z_lo), core: 2. Of those that a mesh axis runs over, the one named last changes fastest.
Arguments:
- latents: bfloat16 [49152, 320], P('dp'), may hold values from -6 to 6
- clip_of_row: int32 [128, 384], P('dp'), may hold values from 0 to 3, never falling along the last dimension, each value on 1 to 192 neighbouring positions
- timestep: int32 [128, 4], P('dp'), may hold values from 0 to 999
- w_in: bfloat16 [6, 320, 640], P('pipe'), may hold values from -0.3125 to 0.3125
- w_out: bfloat16 [6, 640, 320], P('pipe'), may hold values from -0.25 to 0.25
- w_mix: bfloat16 [6, 640, 320], P('pipe'), may hold values from -0.25 to 0.25
- w_up: bfloat16 [6, 320, 320], P('pipe'), may hold values from -0.3125 to 0.3125
- out_grad: bfloat16 [49152, 320], P('dp'), may hold values from -6 to 6
Outputs:
- w_in_grad: float32 [6, 320, 640], P('pipe')
- w_out_grad: float32 [6, 640, 320], P('pipe')
- w_mix_grad: float32 [6, 640, 320], P('pipe')
- w_up_grad: float32 [6, 320, 320], P('pipe')
The draws below stay inside these ranges and needn't reach their ends.
Inputs may be any that keep to these rules, and one draw needn't show every extreme that they name: `clip_of_row`: along each replica's rows the clip numbers never fall; every clip has 1 to 192 rows, and one has exactly 192.
All inputs are finite; a program needn't handle non-finite values.
Results may differ from the reference program's by a relative error of at most 0.019.
Values may be sent and summed in bfloat16 or wider, within the bound.
No kernel may reach another device: no remote copies, remote signals or barrier semaphores. Data moves between devices by JAX's collectives and lax.ppermute only.
A program may use at most 32 MiB of HBM per device.

```python
import math
import jax
import jax.numpy as jnp
import numpy as np
from jax import lax

C = 320
FFN = 640
HIDDEN_SIZE = 640
CLIP_DEV = 4
TIMESTEPS = 1000
ROWS_DEV = 384
TOKENS = 49152
N_DP = 128
N_PIPE = 6


def with_ends(drawn, rng, smallest, high):
    dims = drawn.shape
    index_at = [jax.random.randint(jax.random.fold_in(rng, axis), (), 0, dims[axis]) for axis in range(len(dims))]
    drawn = drawn.at[tuple(index_at)].set(smallest)
    longest = dims.index(max(dims))
    index_at[longest] = (index_at[longest] + 1) % dims[longest]
    return drawn.at[tuple(index_at)].set(high)


def shard_levels(key, shape, pieces, smallest, largest):
    factor_of, own = 1.0, jax.random.fold_in(key, 6)
    for position, blocks in pieces:
        heights = jnp.exp(jax.random.uniform(jax.random.fold_in(own, position), (blocks,), jnp.float32, smallest / len(pieces), largest / len(pieces)))
        factor_of = factor_of * jnp.repeat(heights, shape[position] // blocks).reshape([-1 if axis == position else 1 for axis in range(len(shape))])
    return factor_of


def split_up(amount, total, limit, slope):
    portions = [(1 << 20) // math.isqrt(standing ** slope) + 1 for standing in range(2, amount + 1)]
    rest, given = total - limit - (amount - 1), [1] * (amount - 1)
    while rest > 0:
        free = [i for i in range(amount - 1) if given[i] < limit]
        mass, remaining = sum([portions[i] for i in free]), rest
        for i in free:
            extra = min(limit - given[i], max(1, remaining * portions[i] // mass), rest)
            given[i] = given[i] + extra
            rest = rest - extra
    return np.array([limit] + given)


def ragged(own_key, number_of, total, reach, slope):
    if number_of == 2:
        one = jax.random.randint(own_key, (), max(1, total - reach), min(reach, total - 1) + 1)
        return jnp.stack([one, total - one])
    tallies = jnp.asarray(split_up(number_of, total, reach, slope), jnp.int32)
    pairs = (number_of - 1) // 2
    donor, receiver = tallies[1:1 + 2 * pairs:2], tallies[2:2 + 2 * pairs:2]
    slack = jnp.minimum(donor - 1, reach - receiver)
    passed = jax.random.randint(jax.random.fold_in(own_key, 1), (pairs,), 0, 1 << 20) % (slack + 1)
    tallies = tallies.at[1:1 + 2 * pairs:2].set(donor - passed).at[2:2 + 2 * pairs:2].set(receiver + passed)
    return tallies[jax.random.permutation(jax.random.fold_in(own_key, 2), number_of)]


def centred(key, dims, deviation, bound, shards=(), kind=jnp.bfloat16):
    level = shard_levels(key, dims, shards, -0.22, 0.18) if shards else 1.0
    values = jax.random.normal(key, dims, jnp.float32) * deviation * level
    return jnp.minimum(jnp.maximum(values, -bound), bound).astype(kind)


def setup_inputs(seed: int = 0) -> dict:
    streams_of = jax.random.split(jax.random.key(seed), 9)
    latents = centred(streams_of[0], (TOKENS, C), 1.0, 6.0, ((0, 128),))
    clip_of_row = jax.vmap(lambda own: jnp.searchsorted(jnp.cumsum(ragged(own, CLIP_DEV, ROWS_DEV, ROWS_DEV // 2, 0)), jnp.arange(ROWS_DEV), side="right"))(jax.random.split(streams_of[1], N_DP)).reshape((N_DP, ROWS_DEV)).astype(jnp.int32)
    timestep = with_ends(jax.random.randint(streams_of[2], (N_DP, CLIP_DEV), 0, TIMESTEPS), jax.random.fold_in(streams_of[2], 1), 0, TIMESTEPS - 1).astype(jnp.int32)
    w_in = centred(streams_of[3], (N_PIPE, C, FFN), C ** -0.5, 0.3125, ((0, 6),))
    w_out = centred(streams_of[4], (N_PIPE, FFN, C), FFN ** -0.5, 0.25, ((0, 6),))
    w_mix = centred(streams_of[5], (N_PIPE, HIDDEN_SIZE, C), HIDDEN_SIZE ** -0.5, 0.25, ((0, 6),))
    w_up = centred(streams_of[6], (N_PIPE, C, C), C ** -0.5, 0.3125, ((0, 6),))
    out_grad = centred(streams_of[7], (TOKENS, C), 1.0, 6.0, ((0, 128),))
    return {"latents": latents, "clip_of_row": clip_of_row, "timestep": timestep, "w_in": w_in, "w_out": w_out, "w_mix": w_mix, "w_up": w_up, "out_grad": out_grad}


def rows_product(left, right):
    return lax.dot_general(left, right, (((0,), (0,)), ((), ())), preferred_element_type=jnp.float32)

def times_transposed(left, right):
    return lax.dot_general(left, right, (((1,), (1,)), ((), ())), preferred_element_type=jnp.float32)

def rms_scale(values):
    return lax.rsqrt(lax.optimization_barrier(jnp.mean(values * values, axis=-1, keepdims=True)) + 1e-05)

def silu_slope(values):
    sigma = jax.nn.sigmoid(values)
    return sigma * (1.0 + values * (1.0 - sigma))

def embed(moment, width):
    half = width // 2
    freq = jnp.exp(-math.log(10000.0) * jnp.arange(half, dtype=jnp.float32) / half)
    angle = moment[:, None] * freq[None, :]
    return jnp.concatenate([jnp.sin(angle), jnp.cos(angle)], axis=-1)

def down_forward(hidden, embedding, in_matrix, out_matrix):
    lifted = hidden.astype(jnp.float32) + embedding
    normed = lifted * rms_scale(lifted)
    inner = jnp.dot(normed.astype(jnp.bfloat16), in_matrix, preferred_element_type=jnp.float32)
    gated = jax.nn.silu(inner).astype(jnp.bfloat16)
    return (lifted + jnp.dot(gated, out_matrix, preferred_element_type=jnp.float32)).astype(jnp.bfloat16)

def down_backward(hidden, embedding, in_matrix, out_matrix, cotan):
    lifted = hidden.astype(jnp.float32) + embedding
    scale = rms_scale(lifted)
    normed = lifted * scale
    normed_b = normed.astype(jnp.bfloat16)
    inner = jnp.dot(normed_b, in_matrix, preferred_element_type=jnp.float32)
    gated = jax.nn.silu(inner).astype(jnp.bfloat16)
    grad_out = rows_product(gated, cotan)
    d_gated = times_transposed(cotan, out_matrix)
    d_inner = (d_gated * silu_slope(inner)).astype(jnp.bfloat16)
    grad_in = rows_product(normed_b, d_inner)
    d_normed = times_transposed(d_inner, in_matrix)
    d_lifted = cotan.astype(jnp.float32) + scale * (d_normed - normed * lax.optimization_barrier(jnp.mean(d_normed * normed, axis=-1, keepdims=True)))
    return (d_lifted.astype(jnp.bfloat16), grad_in, grad_out)

def up_forward(below, side, mix_matrix, up_matrix):
    joined = jnp.concatenate([below, side], axis=-1)
    mixed = jnp.dot(joined, mix_matrix, preferred_element_type=jnp.float32)
    normed = mixed * rms_scale(mixed)
    active = jax.nn.silu(normed).astype(jnp.bfloat16)
    return (mixed + jnp.dot(active, up_matrix, preferred_element_type=jnp.float32)).astype(jnp.bfloat16)

def up_backward(below, side, mix_matrix, up_matrix, cotan):
    width = below.shape[-1]
    joined = jnp.concatenate([below, side], axis=-1)
    mixed = jnp.dot(joined, mix_matrix, preferred_element_type=jnp.float32)
    scale = rms_scale(mixed)
    normed = mixed * scale
    active = jax.nn.silu(normed).astype(jnp.bfloat16)
    grad_up = rows_product(active, cotan)
    d_active = times_transposed(cotan, up_matrix)
    d_normed = d_active * silu_slope(normed)
    d_mixed = (cotan.astype(jnp.float32) + scale * (d_normed - normed * lax.optimization_barrier(jnp.mean(d_normed * normed, axis=-1, keepdims=True)))).astype(jnp.bfloat16)
    grad_mix = rows_product(joined, d_mixed)
    d_joined = times_transposed(d_mixed, mix_matrix)
    return (d_joined[:, :width].astype(jnp.bfloat16), d_joined[:, width:], grad_mix, grad_up)

def reference(latents, clip_of_row, timestep, w_in, w_out, w_mix, w_up, out_grad):
    moment = jnp.take_along_axis(timestep, clip_of_row, axis=1).reshape(-1).astype(jnp.float32)
    embedding = embed(moment, C)
    sections = N_PIPE
    down_inputs = []
    skips = []
    hidden = latents
    for index in range(sections):
        down_inputs.append(hidden)
        hidden = down_forward(hidden, embedding, w_in[index], w_out[index])
        skips.append(hidden)
    up_inputs = [None] * sections
    below = skips[-1]
    for index in range(sections - 1, -1, -1):
        up_inputs[index] = below
        below = up_forward(below, skips[index], w_mix[index], w_up[index])
    cotan = out_grad
    sides = [None] * sections
    mix_grads = [None] * sections
    up_grads = [None] * sections
    for index in range(sections):
        cotan, sides[index], mix_grads[index], up_grads[index] = up_backward(up_inputs[index], skips[index], w_mix[index], w_up[index], cotan)
    carry = cotan.astype(jnp.float32)
    in_grads = [None] * sections
    out_grads = [None] * sections
    for index in range(sections - 1, -1, -1):
        total = (carry + sides[index]).astype(jnp.bfloat16)
        d_hidden, in_grads[index], out_grads[index] = down_backward(down_inputs[index], embedding, w_in[index], w_out[index], total)
        carry = d_hidden.astype(jnp.float32)
    factor = 1.0 / N_DP
    return (jnp.stack(in_grads) * factor, jnp.stack(out_grads) * factor, jnp.stack(mix_grads) * factor, jnp.stack(up_grads) * factor)
```

```python
import math

import jax
import jax.numpy as jnp
from jax import lax
from jax.sharding import Mesh, PartitionSpec as P

MICRO = 4
DP = ("y", "x", "zl")


def shifted(value, axis, steps):
    count = lax.axis_size(axis)
    leading, last = (max(0, -steps), min(count, count - steps))
    return lax.ppermute(value, axis, [(source, source + steps) for source in range(leading, last)])


def rows_product(left, right):
    return lax.dot_general(
        left, right, (((0,), (0,)), ((), ())), preferred_element_type=jnp.float32
    )


def times_transposed(left, right):
    return lax.dot_general(
        left, right, (((1,), (1,)), ((), ())), preferred_element_type=jnp.float32
    )


def rms_scale(values):
    return lax.rsqrt(jnp.mean(values * values, axis=-1, keepdims=True) + 1e-05)


def silu_slope(values):
    sigma = jax.nn.sigmoid(values)
    return sigma * (1.0 + values * (1.0 - sigma))


def embed(moment, width):
    half = width // 2
    freq = jnp.exp(-math.log(10000.0) * jnp.arange(half, dtype=jnp.float32) / half)
    angle = moment[:, None] * freq[None, :]
    return jnp.concatenate([jnp.sin(angle), jnp.cos(angle)], axis=-1)


def down_forward(hidden, embedding, in_matrix, out_matrix):
    lifted = hidden.astype(jnp.float32) + embedding
    normed = lifted * rms_scale(lifted)
    inner = jnp.dot(normed.astype(jnp.bfloat16), in_matrix, preferred_element_type=jnp.float32)
    gated = jax.nn.silu(inner).astype(jnp.bfloat16)
    return (lifted + jnp.dot(gated, out_matrix, preferred_element_type=jnp.float32)).astype(
        jnp.bfloat16
    )


def down_backward(hidden, embedding, in_matrix, out_matrix, cotan):
    lifted = hidden.astype(jnp.float32) + embedding
    scale = rms_scale(lifted)
    normed = lifted * scale
    normed_b = normed.astype(jnp.bfloat16)
    inner = jnp.dot(normed_b, in_matrix, preferred_element_type=jnp.float32)
    gated = jax.nn.silu(inner).astype(jnp.bfloat16)
    grad_out = rows_product(gated, cotan)
    d_gated = times_transposed(cotan, out_matrix)
    d_inner = (d_gated * silu_slope(inner)).astype(jnp.bfloat16)
    grad_in = rows_product(normed_b, d_inner)
    d_normed = times_transposed(d_inner, in_matrix)
    d_lifted = cotan.astype(jnp.float32) + scale * (
        d_normed - normed * jnp.mean(d_normed * normed, axis=-1, keepdims=True)
    )
    return (d_lifted.astype(jnp.bfloat16), grad_in, grad_out)


def up_forward(below, side, mix_matrix, up_matrix):
    joined = jnp.concatenate([below, side], axis=-1)
    mixed = jnp.dot(joined, mix_matrix, preferred_element_type=jnp.float32)
    normed = mixed * rms_scale(mixed)
    active = jax.nn.silu(normed).astype(jnp.bfloat16)
    return (mixed + jnp.dot(active, up_matrix, preferred_element_type=jnp.float32)).astype(
        jnp.bfloat16
    )


def up_backward(below, side, mix_matrix, up_matrix, cotan):
    width = below.shape[-1]
    joined = jnp.concatenate([below, side], axis=-1)
    mixed = jnp.dot(joined, mix_matrix, preferred_element_type=jnp.float32)
    scale = rms_scale(mixed)
    normed = mixed * scale
    active = jax.nn.silu(normed).astype(jnp.bfloat16)
    grad_up = rows_product(active, cotan)
    d_active = times_transposed(cotan, up_matrix)
    d_normed = d_active * silu_slope(normed)
    d_mixed = (
        cotan.astype(jnp.float32)
        + scale * (d_normed - normed * jnp.mean(d_normed * normed, axis=-1, keepdims=True))
    ).astype(jnp.bfloat16)
    grad_mix = rows_product(joined, d_mixed)
    d_joined = times_transposed(d_mixed, mix_matrix)
    return (d_joined[:, :width].astype(jnp.bfloat16), d_joined[:, width:], grad_mix, grad_up)


def pick(store, slot):
    return lax.dynamic_index_in_dim(store, slot, 0, keepdims=False)


def place(store, slot, value, valid):
    return lax.dynamic_update_index_in_dim(
        store, jnp.where(valid, value, pick(store, slot)), slot, 0
    )


def run_ticks(lower, upper, step, carry):
    return lax.fori_loop(lower, upper, lambda tick, state: step(state, tick), carry)


def reduce_replicas(parts):
    total = sum(part.size for part in parts)
    groups = math.prod(lax.axis_size(name) for name in DP)
    lanes = 128
    length = -(-total // (lanes * groups * 8)) * groups * 8
    flat = jnp.concatenate([part.reshape(-1) for part in parts])
    flat = jnp.pad(flat, (0, length * lanes - total)).reshape(length, lanes)
    for name in reversed(DP):
        flat = lax.psum_scatter(flat, name, scatter_dimension=0, tiled=True)
    for name in DP:
        flat = lax.all_gather(flat, name, axis=0, tiled=True)
    flat = flat.reshape(-1)
    out, start = [], 0
    for part in parts:
        out.append(flat[start : start + part.size].reshape(part.shape))
        start += part.size
    return tuple(out)


def dp_split(mesh):
    column = mesh.devices[:, 0]
    sizes = [len({int(device.coords[axis]) for device in column}) for axis in (1, 0, 2)]
    if math.prod(sizes) != column.size:
        raise ValueError("dp split")
    return tuple(sizes)


def local(latents, clip_of_row, timestep, w_in, w_out, w_mix, w_up, out_grad):
    sections = lax.axis_size("pipe")
    section = lax.axis_index("pipe")
    width = latents.shape[1]
    micro = MICRO
    rows = latents.shape[0] // micro
    span = micro + sections - 1
    in_matrix = w_in[0]
    out_matrix = w_out[0]
    mix_matrix = w_mix[0]
    up_matrix = w_up[0]
    match = clip_of_row[0][:, None] == jnp.arange(timestep.shape[1], dtype=jnp.int32)[None, :]
    moment = jnp.sum(jnp.where(match, timestep[0][None, :], 0), axis=1).astype(jnp.float32)
    embedding = embed(moment, width)
    input_blocks = latents.reshape(micro, rows, width)
    embed_blocks = embedding.reshape(micro, rows, width)
    grad_blocks = out_grad.reshape(micro, rows, width)
    plain = jnp.zeros((rows, width), jnp.bfloat16)
    blank = jnp.zeros((micro, rows, width), jnp.bfloat16)

    def position(tick, offset):
        batch = tick - offset
        valid = (batch >= 0) & (batch < micro)
        return (jnp.clip(batch, 0, micro - 1), valid)

    def down_tick(carry, tick):
        recv_down, recv_up, down_in, skip, up_in = carry
        slot, valid = position(tick, section)
        source = jnp.where(section == 0, pick(input_blocks, slot), recv_down)
        result = lax.cond(
            valid,
            lambda: down_forward(source, pick(embed_blocks, slot), in_matrix, out_matrix),
            lambda: plain,
        )
        down_in = place(down_in, slot, source, valid)
        skip = place(skip, slot, result, valid)
        recv_down = shifted(result, "pipe", 1)
        return (recv_down, recv_up, down_in, skip, up_in)

    def up_tick(carry, tick):
        recv_down, recv_up, down_in, skip, up_in = carry
        slot, valid = position(tick, sections - 1 - section)
        side = pick(skip, slot)
        below = jnp.where(section == sections - 1, side, recv_up)
        result = lax.cond(
            valid, lambda: up_forward(below, side, mix_matrix, up_matrix), lambda: plain
        )
        up_in = place(up_in, slot, below, valid)
        recv_up = shifted(result, "pipe", -1)
        return (recv_down, recv_up, down_in, skip, up_in)

    forward = (plain, plain, blank, blank, blank)
    forward = run_ticks(0, span, down_tick, forward)
    forward = run_ticks(0, span, up_tick, forward)
    down_in, skip, up_in = (forward[2], forward[3], forward[4])
    zero_in = jnp.zeros(in_matrix.shape, jnp.float32)
    zero_out = jnp.zeros(out_matrix.shape, jnp.float32)
    zero_mix = jnp.zeros(mix_matrix.shape, jnp.float32)
    zero_up = jnp.zeros(up_matrix.shape, jnp.float32)
    zero_side = jnp.zeros((rows, width), jnp.float32)

    def up_back_tick(carry, tick):
        recv_up, recv_down, d_skip, grad_in, grad_out, grad_mix, grad_up = carry
        slot, valid = position(tick, section)
        cotan = jnp.where(section == 0, pick(grad_blocks, slot), recv_up)
        d_below, d_side, part_mix, part_up = lax.cond(
            valid,
            lambda: up_backward(pick(up_in, slot), pick(skip, slot), mix_matrix, up_matrix, cotan),
            lambda: (plain, zero_side, zero_mix, zero_up),
        )
        side_total = d_side + jnp.where(section == sections - 1, d_below.astype(jnp.float32), 0.0)
        d_skip = place(d_skip, slot, side_total, valid)
        recv_up = shifted(d_below, "pipe", 1)
        return (
            recv_up,
            recv_down,
            d_skip,
            grad_in,
            grad_out,
            grad_mix + part_mix,
            grad_up + part_up,
        )

    def down_back_tick(carry, tick):
        recv_up, recv_down, d_skip, grad_in, grad_out, grad_mix, grad_up = carry
        slot, valid = position(tick, sections - 1 - section)
        cotan = (pick(d_skip, slot) + recv_down.astype(jnp.float32)).astype(jnp.bfloat16)
        d_hidden, part_in, part_out = lax.cond(
            valid,
            lambda: down_backward(
                pick(down_in, slot), pick(embed_blocks, slot), in_matrix, out_matrix, cotan
            ),
            lambda: (plain, zero_in, zero_out),
        )
        recv_down = shifted(d_hidden, "pipe", -1)
        return (
            recv_up,
            recv_down,
            d_skip,
            grad_in + part_in,
            grad_out + part_out,
            grad_mix,
            grad_up,
        )

    backward = (
        plain,
        plain,
        jnp.zeros((micro, rows, width), jnp.float32),
        zero_in,
        zero_out,
        zero_mix,
        zero_up,
    )
    backward = run_ticks(0, span, up_back_tick, backward)
    backward = run_ticks(0, span, down_back_tick, backward)
    grad_in, grad_out, grad_mix, grad_up = reduce_replicas(
        (backward[3], backward[4], backward[5], backward[6])
    )
    factor = 1.0 / math.prod(lax.axis_size(name) for name in DP)
    return (
        (grad_in * factor)[None],
        (grad_out * factor)[None],
        (grad_mix * factor)[None],
        (grad_up * factor)[None],
    )


def solution(mesh):
    sizes = dp_split(mesh)
    pipe = mesh.devices.shape[1]
    split = Mesh(mesh.devices.reshape(*sizes, pipe), DP + ("pipe",))
    return jax.shard_map(
        local,
        mesh=split,
        in_specs=(
            P(DP, None),
            P(DP, None),
            P(DP, None),
            P("pipe", None, None),
            P("pipe", None, None),
            P("pipe", None, None),
            P("pipe", None, None),
            P(DP, None),
        ),
        out_specs=(
            P("pipe", None, None),
            P("pipe", None, None),
            P("pipe", None, None),
            P("pipe", None, None),
        ),
        check_vma=False,
    )
```

```python
import math

import jax
import jax.numpy as jnp
from jax import lax
from jax.sharding import Mesh, PartitionSpec as P

DP = ("y", "x", "zl")
SCATTER = ("y", "x", "zl")


def rows_product(left, right):
    return lax.dot_general(
        left, right, (((0,), (0,)), ((), ())), preferred_element_type=jnp.float32
    )


def times_transposed(left, right):
    return lax.dot_general(
        left, right, (((1,), (1,)), ((), ())), preferred_element_type=jnp.float32
    )


def rms_scale(values):
    return lax.rsqrt(jnp.mean(values * values, axis=-1, keepdims=True) + 1e-05)


def silu_slope(values):
    sigma = jax.nn.sigmoid(values)
    return sigma * (1.0 + values * (1.0 - sigma))


def embed(moment, width):
    half = width // 2
    freq = jnp.exp(-math.log(10000.0) * jnp.arange(half, dtype=jnp.float32) / half)
    angle = moment[:, None] * freq[None, :]
    return jnp.concatenate([jnp.sin(angle), jnp.cos(angle)], axis=-1)


def down_forward(hidden, embedding, in_matrix, out_matrix):
    lifted = hidden.astype(jnp.float32) + embedding
    normed = lifted * rms_scale(lifted)
    inner = jnp.dot(normed.astype(jnp.bfloat16), in_matrix, preferred_element_type=jnp.float32)
    gated = jax.nn.silu(inner).astype(jnp.bfloat16)
    return (lifted + jnp.dot(gated, out_matrix, preferred_element_type=jnp.float32)).astype(
        jnp.bfloat16
    )


def down_backward(hidden, embedding, in_matrix, out_matrix, cotan):
    lifted = hidden.astype(jnp.float32) + embedding
    scale = rms_scale(lifted)
    normed = lifted * scale
    normed_b = normed.astype(jnp.bfloat16)
    inner = jnp.dot(normed_b, in_matrix, preferred_element_type=jnp.float32)
    gated = jax.nn.silu(inner).astype(jnp.bfloat16)
    grad_out = rows_product(gated, cotan)
    d_gated = times_transposed(cotan, out_matrix)
    d_inner = (d_gated * silu_slope(inner)).astype(jnp.bfloat16)
    grad_in = rows_product(normed_b, d_inner)
    d_normed = times_transposed(d_inner, in_matrix)
    d_lifted = cotan.astype(jnp.float32) + scale * (
        d_normed - normed * jnp.mean(d_normed * normed, axis=-1, keepdims=True)
    )
    return (d_lifted.astype(jnp.bfloat16), grad_in, grad_out)


def up_forward(below, side, mix_matrix, up_matrix):
    joined = jnp.concatenate([below, side], axis=-1)
    mixed = jnp.dot(joined, mix_matrix, preferred_element_type=jnp.float32)
    normed = mixed * rms_scale(mixed)
    active = jax.nn.silu(normed).astype(jnp.bfloat16)
    return (mixed + jnp.dot(active, up_matrix, preferred_element_type=jnp.float32)).astype(
        jnp.bfloat16
    )


def up_backward(below, side, mix_matrix, up_matrix, cotan):
    width = below.shape[-1]
    joined = jnp.concatenate([below, side], axis=-1)
    mixed = jnp.dot(joined, mix_matrix, preferred_element_type=jnp.float32)
    scale = rms_scale(mixed)
    normed = mixed * scale
    active = jax.nn.silu(normed).astype(jnp.bfloat16)
    grad_up = rows_product(active, cotan)
    d_active = times_transposed(cotan, up_matrix)
    d_normed = d_active * silu_slope(normed)
    d_mixed = (
        cotan.astype(jnp.float32)
        + scale * (d_normed - normed * jnp.mean(d_normed * normed, axis=-1, keepdims=True))
    ).astype(jnp.bfloat16)
    grad_mix = rows_product(joined, d_mixed)
    d_joined = times_transposed(d_mixed, mix_matrix)
    return (d_joined[:, :width].astype(jnp.bfloat16), d_joined[:, width:], grad_mix, grad_up)


def reduce_replicas(parts):
    total = sum(part.size for part in parts)
    groups = math.prod(lax.axis_size(name) for name in DP)
    lanes = 128
    length = -(-total // (lanes * groups * 8)) * groups * 8
    flat = jnp.concatenate([part.reshape(-1) for part in parts])
    flat = jnp.pad(flat, (0, length * lanes - total)).reshape(length, lanes)
    for name in SCATTER:
        flat = lax.psum_scatter(flat, name, scatter_dimension=0, tiled=True)
    for name in reversed(SCATTER):
        flat = lax.all_gather(flat, name, axis=0, tiled=True)
    flat = flat.reshape(-1)
    out, start = [], 0
    for part in parts:
        out.append(flat[start : start + part.size].reshape(part.shape))
        start += part.size
    return tuple(out)


def dp_split(mesh):
    column = mesh.devices[:, 0]
    sizes = [len({int(device.coords[axis]) for device in column}) for axis in (1, 0, 2)]
    if math.prod(sizes) != column.size:
        raise ValueError("dp split")
    return tuple(sizes)


def swap_core(value):
    return lax.ppermute(value, "core", [(0, 1), (1, 0)])


def hop(value, source, target):
    return lax.ppermute(value, "zh", [(source, target)])


def keep(valid, new, old):
    return new if old is None else jnp.where(valid, new, old)


def local(latents, clip_of_row, timestep, w_in, w_out, w_mix, w_up, out_grad):
    stages = lax.axis_size("zh")
    stage = lax.axis_index("zh")
    core = lax.axis_index("core")
    first = core == 0
    width = latents.shape[1]
    rows = latents.shape[0] // lax.axis_size("core")

    def pair(weights):
        own = weights[0]
        other = swap_core(own)
        return (jnp.where(first, own, other), jnp.where(first, other, own))

    in_pair, out_pair = pair(w_in), pair(w_out)
    mix_pair, up_pair = pair(w_mix), pair(w_up)

    offset = core * rows
    match = clip_of_row[0][:, None] == jnp.arange(timestep.shape[1], dtype=jnp.int32)[None, :]
    moment = jnp.sum(jnp.where(match, timestep[0][None, :], 0), axis=1).astype(jnp.float32)
    moment = lax.dynamic_slice_in_dim(moment, offset, rows)
    embedding = embed(moment, width)
    source = lax.dynamic_slice_in_dim(latents, offset, rows)
    seed = lax.dynamic_slice_in_dim(out_grad, offset, rows)

    down_in = [None, None]
    skip = [None, None]
    hidden = source
    for tick in range(stages):
        if tick > 0:
            hidden = hop(hidden, tick - 1, tick)
        valid = stage == tick
        lower = hidden
        upper = down_forward(lower, embedding, in_pair[0], out_pair[0])
        hidden = down_forward(upper, embedding, in_pair[1], out_pair[1])
        down_in = [keep(valid, lower, down_in[0]), keep(valid, upper, down_in[1])]
        skip = [keep(valid, upper, skip[0]), keep(valid, hidden, skip[1])]

    up_in = [None, None]
    below = skip[1]
    for tick in range(stages):
        owner = stages - 1 - tick
        if tick > 0:
            below = hop(below, owner + 1, owner)
        valid = stage == owner
        middle = up_forward(below, skip[1], mix_pair[1], up_pair[1])
        up_in = [keep(valid, middle, up_in[0]), keep(valid, below, up_in[1])]
        below = up_forward(middle, skip[0], mix_pair[0], up_pair[0])

    d_skip = [None, None]
    grad_mix = [None, None]
    grad_up = [None, None]
    cotan = seed
    for tick in range(stages):
        if tick > 0:
            cotan = hop(cotan, tick - 1, tick)
        valid = stage == tick
        middle, side0, mix0, up0 = up_backward(up_in[0], skip[0], mix_pair[0], up_pair[0], cotan)
        cotan, side1, mix1, up1 = up_backward(up_in[1], skip[1], mix_pair[1], up_pair[1], middle)
        d_skip = [keep(valid, side0, d_skip[0]), keep(valid, side1, d_skip[1])]
        grad_mix = [keep(valid, mix0, grad_mix[0]), keep(valid, mix1, grad_mix[1])]
        grad_up = [keep(valid, up0, grad_up[0]), keep(valid, up1, grad_up[1])]

    def combine(grads):
        mine = jnp.where(first, grads[0], grads[1])
        theirs = jnp.where(first, grads[1], grads[0])
        return mine + swap_core(theirs)

    factor = 1.0 / math.prod(lax.axis_size(name) for name in DP)
    total_mix, total_up = reduce_replicas((combine(grad_mix), combine(grad_up)))

    grad_in = [None, None]
    grad_out = [None, None]
    carry = cotan
    for tick in range(stages):
        owner = stages - 1 - tick
        if tick > 0:
            carry = hop(carry, owner + 1, owner)
        valid = stage == owner
        upper_c = (d_skip[1] + carry.astype(jnp.float32)).astype(jnp.bfloat16)
        upper_d, in1, out1 = down_backward(down_in[1], embedding, in_pair[1], out_pair[1], upper_c)
        lower_c = (d_skip[0] + upper_d.astype(jnp.float32)).astype(jnp.bfloat16)
        carry, in0, out0 = down_backward(down_in[0], embedding, in_pair[0], out_pair[0], lower_c)
        grad_in = [keep(valid, in0, grad_in[0]), keep(valid, in1, grad_in[1])]
        grad_out = [keep(valid, out0, grad_out[0]), keep(valid, out1, grad_out[1])]

    total_in, total_out = reduce_replicas((combine(grad_in), combine(grad_out)))
    return (
        (total_in * factor)[None],
        (total_out * factor)[None],
        (total_mix * factor)[None],
        (total_up * factor)[None],
    )


def solution(mesh):
    sizes = dp_split(mesh)
    pipe = mesh.devices.shape[1]
    split = Mesh(mesh.devices.reshape(*sizes, pipe // 2, 2), DP + ("zh", "core"))
    sections = ("zh", "core")
    return jax.shard_map(
        local,
        mesh=split,
        in_specs=(
            P(DP, None),
            P(DP, None),
            P(DP, None),
            P(sections, None, None),
            P(sections, None, None),
            P(sections, None, None),
            P(sections, None, None),
            P(DP, None),
        ),
        out_specs=(
            P(sections, None, None),
            P(sections, None, None),
            P(sections, None, None),
            P(sections, None, None),
        ),
        check_vma=False,
    )
```

```python
import math

import jax
import jax.numpy as jnp
from jax import lax
from jax.sharding import Mesh, PartitionSpec as P

DP = ("y", "x", "zl")
SCATTER = ("y", "x", "zl")


def rows_product(left, right):
    return lax.dot_general(
        left, right, (((0,), (0,)), ((), ())), preferred_element_type=jnp.float32
    )


def times_transposed(left, right):
    return lax.dot_general(
        left, right, (((1,), (1,)), ((), ())), preferred_element_type=jnp.float32
    )


def rms_scale(values):
    return lax.rsqrt(jnp.mean(values * values, axis=-1, keepdims=True) + 1e-05)


def silu_slope(values):
    sigma = jax.nn.sigmoid(values)
    return sigma * (1.0 + values * (1.0 - sigma))


def embed(moment, width):
    half = width // 2
    freq = jnp.exp(-math.log(10000.0) * jnp.arange(half, dtype=jnp.float32) / half)
    angle = moment[:, None] * freq[None, :]
    return jnp.concatenate([jnp.sin(angle), jnp.cos(angle)], axis=-1)


def down_forward(hidden, embedding, in_matrix, out_matrix):
    lifted = hidden.astype(jnp.float32) + embedding
    normed = lifted * rms_scale(lifted)
    inner = jnp.dot(normed.astype(jnp.bfloat16), in_matrix, preferred_element_type=jnp.float32)
    gated = jax.nn.silu(inner).astype(jnp.bfloat16)
    return (lifted + jnp.dot(gated, out_matrix, preferred_element_type=jnp.float32)).astype(
        jnp.bfloat16
    )


def down_backward(hidden, embedding, in_matrix, out_matrix, cotan):
    lifted = hidden.astype(jnp.float32) + embedding
    scale = rms_scale(lifted)
    normed = lifted * scale
    normed_b = normed.astype(jnp.bfloat16)
    inner = jnp.dot(normed_b, in_matrix, preferred_element_type=jnp.float32)
    gated = jax.nn.silu(inner).astype(jnp.bfloat16)
    grad_out = rows_product(gated, cotan)
    d_gated = times_transposed(cotan, out_matrix)
    d_inner = (d_gated * silu_slope(inner)).astype(jnp.bfloat16)
    grad_in = rows_product(normed_b, d_inner)
    d_normed = times_transposed(d_inner, in_matrix)
    d_lifted = cotan.astype(jnp.float32) + scale * (
        d_normed - normed * jnp.mean(d_normed * normed, axis=-1, keepdims=True)
    )
    return (d_lifted.astype(jnp.bfloat16), grad_in, grad_out)


def up_forward(below, side, mix_matrix, up_matrix):
    joined = jnp.concatenate([below, side], axis=-1)
    mixed = jnp.dot(joined, mix_matrix, preferred_element_type=jnp.float32)
    normed = mixed * rms_scale(mixed)
    active = jax.nn.silu(normed).astype(jnp.bfloat16)
    return (mixed + jnp.dot(active, up_matrix, preferred_element_type=jnp.float32)).astype(
        jnp.bfloat16
    )


def up_backward(below, side, mix_matrix, up_matrix, cotan):
    width = below.shape[-1]
    joined = jnp.concatenate([below, side], axis=-1)
    mixed = jnp.dot(joined, mix_matrix, preferred_element_type=jnp.float32)
    scale = rms_scale(mixed)
    normed = mixed * scale
    active = jax.nn.silu(normed).astype(jnp.bfloat16)
    grad_up = rows_product(active, cotan)
    d_active = times_transposed(cotan, up_matrix)
    d_normed = d_active * silu_slope(normed)
    d_mixed = (
        cotan.astype(jnp.float32)
        + scale * (d_normed - normed * jnp.mean(d_normed * normed, axis=-1, keepdims=True))
    ).astype(jnp.bfloat16)
    grad_mix = rows_product(joined, d_mixed)
    d_joined = times_transposed(d_mixed, mix_matrix)
    return (d_joined[:, :width].astype(jnp.bfloat16), d_joined[:, width:], grad_mix, grad_up)


def reduce_replicas(parts):
    total = sum(part.size for part in parts)
    groups = math.prod(lax.axis_size(name) for name in DP)
    lanes = 128
    length = -(-total // (lanes * groups * 8)) * groups * 8
    flat = jnp.concatenate([part.reshape(-1) for part in parts])
    flat = jnp.pad(flat, (0, length * lanes - total)).reshape(length, lanes)
    flat = lax.psum(flat, ("y", "x"))
    flat = lax.psum(flat, "zl")
    flat = flat.reshape(-1)
    out, start = [], 0
    for part in parts:
        out.append(flat[start : start + part.size].reshape(part.shape))
        start += part.size
    return tuple(out)


def dp_split(mesh):
    column = mesh.devices[:, 0]
    sizes = [len({int(device.coords[axis]) for device in column}) for axis in (1, 0, 2)]
    if math.prod(sizes) != column.size:
        raise ValueError("dp split")
    return tuple(sizes)


def swap_core(value):
    return lax.ppermute(value, "core", [(0, 1), (1, 0)])


def hop(value, source, target):
    return lax.ppermute(value, "zh", [(source, target)])


def keep(valid, new, old):
    return new if old is None else jnp.where(valid, new, old)


def local(latents, clip_of_row, timestep, w_in, w_out, w_mix, w_up, out_grad):
    stages = lax.axis_size("zh")
    stage = lax.axis_index("zh")
    core = lax.axis_index("core")
    first = core == 0
    width = latents.shape[1]
    rows = latents.shape[0] // lax.axis_size("core")

    def pair(weights):
        own = weights[0]
        other = swap_core(own)
        return (jnp.where(first, own, other), jnp.where(first, other, own))

    in_pair, out_pair = pair(w_in), pair(w_out)
    mix_pair, up_pair = pair(w_mix), pair(w_up)

    offset = core * rows
    match = clip_of_row[0][:, None] == jnp.arange(timestep.shape[1], dtype=jnp.int32)[None, :]
    moment = jnp.sum(jnp.where(match, timestep[0][None, :], 0), axis=1).astype(jnp.float32)
    moment = lax.dynamic_slice_in_dim(moment, offset, rows)
    embedding = embed(moment, width)
    source = lax.dynamic_slice_in_dim(latents, offset, rows)
    seed = lax.dynamic_slice_in_dim(out_grad, offset, rows)

    down_in = [None, None]
    skip = [None, None]
    hidden = source
    for tick in range(stages):
        if tick > 0:
            hidden = hop(hidden, tick - 1, tick)
        valid = stage == tick
        lower = hidden
        upper = down_forward(lower, embedding, in_pair[0], out_pair[0])
        hidden = down_forward(upper, embedding, in_pair[1], out_pair[1])
        down_in = [keep(valid, lower, down_in[0]), keep(valid, upper, down_in[1])]
        skip = [keep(valid, upper, skip[0]), keep(valid, hidden, skip[1])]

    up_in = [None, None]
    below = skip[1]
    for tick in range(stages):
        owner = stages - 1 - tick
        if tick > 0:
            below = hop(below, owner + 1, owner)
        valid = stage == owner
        middle = up_forward(below, skip[1], mix_pair[1], up_pair[1])
        up_in = [keep(valid, middle, up_in[0]), keep(valid, below, up_in[1])]
        below = up_forward(middle, skip[0], mix_pair[0], up_pair[0])

    d_skip = [None, None]
    grad_mix = [None, None]
    grad_up = [None, None]
    cotan = seed
    for tick in range(stages):
        if tick > 0:
            cotan = hop(cotan, tick - 1, tick)
        valid = stage == tick
        middle, side0, mix0, up0 = up_backward(up_in[0], skip[0], mix_pair[0], up_pair[0], cotan)
        cotan, side1, mix1, up1 = up_backward(up_in[1], skip[1], mix_pair[1], up_pair[1], middle)
        d_skip = [keep(valid, side0, d_skip[0]), keep(valid, side1, d_skip[1])]
        grad_mix = [keep(valid, mix0, grad_mix[0]), keep(valid, mix1, grad_mix[1])]
        grad_up = [keep(valid, up0, grad_up[0]), keep(valid, up1, grad_up[1])]

    def combine(grads):
        mine = jnp.where(first, grads[0], grads[1])
        theirs = jnp.where(first, grads[1], grads[0])
        return mine + swap_core(theirs)

    factor = 1.0 / math.prod(lax.axis_size(name) for name in DP)
    total_mix, total_up = reduce_replicas((combine(grad_mix), combine(grad_up)))

    grad_in = [None, None]
    grad_out = [None, None]
    carry = cotan
    for tick in range(stages):
        owner = stages - 1 - tick
        if tick > 0:
            carry = hop(carry, owner + 1, owner)
        valid = stage == owner
        upper_c = (d_skip[1] + carry.astype(jnp.float32)).astype(jnp.bfloat16)
        upper_d, in1, out1 = down_backward(down_in[1], embedding, in_pair[1], out_pair[1], upper_c)
        lower_c = (d_skip[0] + upper_d.astype(jnp.float32)).astype(jnp.bfloat16)
        carry, in0, out0 = down_backward(down_in[0], embedding, in_pair[0], out_pair[0], lower_c)
        grad_in = [keep(valid, in0, grad_in[0]), keep(valid, in1, grad_in[1])]
        grad_out = [keep(valid, out0, grad_out[0]), keep(valid, out1, grad_out[1])]

    total_in, total_out = reduce_replicas((combine(grad_in), combine(grad_out)))
    return (
        (total_in * factor)[None],
        (total_out * factor)[None],
        (total_mix * factor)[None],
        (total_up * factor)[None],
    )


def solution(mesh):
    sizes = dp_split(mesh)
    pipe = mesh.devices.shape[1]
    split = Mesh(mesh.devices.reshape(*sizes, pipe // 2, 2), DP + ("zh", "core"))
    sections = ("zh", "core")
    return jax.shard_map(
        local,
        mesh=split,
        in_specs=(
            P(DP, None),
            P(DP, None),
            P(DP, None),
            P(sections, None, None),
            P(sections, None, None),
            P(sections, None, None),
            P(sections, None, None),
            P(DP, None),
        ),
        out_specs=(
            P(sections, None, None),
            P(sections, None, None),
            P(sections, None, None),
            P(sections, None, None),
        ),
        check_vma=False,
    )
```

```python
import math

import jax
import jax.numpy as jnp
from jax import lax
from jax.sharding import Mesh, PartitionSpec as P

DP = ("y", "x", "zl")
SCATTER = ("y", "x", "zl")


def rows_product(left, right):
    return lax.dot_general(
        left, right, (((0,), (0,)), ((), ())), preferred_element_type=jnp.float32
    )


def times_transposed(left, right):
    return lax.dot_general(
        left, right, (((1,), (1,)), ((), ())), preferred_element_type=jnp.float32
    )


def rms_scale(values):
    return lax.rsqrt(jnp.mean(values * values, axis=-1, keepdims=True) + 1e-05)


def silu_slope(values):
    sigma = jax.nn.sigmoid(values)
    return sigma * (1.0 + values * (1.0 - sigma))


def embed(moment, width):
    half = width // 2
    freq = jnp.exp(-math.log(10000.0) * jnp.arange(half, dtype=jnp.float32) / half)
    angle = moment[:, None] * freq[None, :]
    return jnp.concatenate([jnp.sin(angle), jnp.cos(angle)], axis=-1)


def down_forward(hidden, embedding, in_matrix, out_matrix):
    lifted = hidden.astype(jnp.float32) + embedding
    normed = lifted * rms_scale(lifted)
    inner = jnp.dot(normed.astype(jnp.bfloat16), in_matrix, preferred_element_type=jnp.float32)
    gated = jax.nn.silu(inner).astype(jnp.bfloat16)
    return (lifted + jnp.dot(gated, out_matrix, preferred_element_type=jnp.float32)).astype(
        jnp.bfloat16
    )


def down_backward(hidden, embedding, in_matrix, out_matrix, cotan):
    lifted = hidden.astype(jnp.float32) + embedding
    scale = rms_scale(lifted)
    normed = lifted * scale
    normed_b = normed.astype(jnp.bfloat16)
    inner = jnp.dot(normed_b, in_matrix, preferred_element_type=jnp.float32)
    gated = jax.nn.silu(inner).astype(jnp.bfloat16)
    grad_out = rows_product(gated, cotan)
    d_gated = times_transposed(cotan, out_matrix)
    d_inner = (d_gated * silu_slope(inner)).astype(jnp.bfloat16)
    grad_in = rows_product(normed_b, d_inner)
    d_normed = times_transposed(d_inner, in_matrix)
    d_lifted = cotan.astype(jnp.float32) + scale * (
        d_normed - normed * jnp.mean(d_normed * normed, axis=-1, keepdims=True)
    )
    return (d_lifted.astype(jnp.bfloat16), grad_in, grad_out)


def up_forward(below, side, mix_matrix, up_matrix):
    joined = jnp.concatenate([below, side], axis=-1)
    mixed = jnp.dot(joined, mix_matrix, preferred_element_type=jnp.float32)
    normed = mixed * rms_scale(mixed)
    active = jax.nn.silu(normed).astype(jnp.bfloat16)
    return (mixed + jnp.dot(active, up_matrix, preferred_element_type=jnp.float32)).astype(
        jnp.bfloat16
    )


def up_backward(below, side, mix_matrix, up_matrix, cotan):
    width = below.shape[-1]
    joined = jnp.concatenate([below, side], axis=-1)
    mixed = jnp.dot(joined, mix_matrix, preferred_element_type=jnp.float32)
    scale = rms_scale(mixed)
    normed = mixed * scale
    active = jax.nn.silu(normed).astype(jnp.bfloat16)
    grad_up = rows_product(active, cotan)
    d_active = times_transposed(cotan, up_matrix)
    d_normed = d_active * silu_slope(normed)
    d_mixed = (
        cotan.astype(jnp.float32)
        + scale * (d_normed - normed * jnp.mean(d_normed * normed, axis=-1, keepdims=True))
    ).astype(jnp.bfloat16)
    grad_mix = rows_product(joined, d_mixed)
    d_joined = times_transposed(d_mixed, mix_matrix)
    return (d_joined[:, :width].astype(jnp.bfloat16), d_joined[:, width:], grad_mix, grad_up)


def reduce_replicas(parts):
    total = sum(part.size for part in parts)
    groups = math.prod(lax.axis_size(name) for name in DP)
    lanes = 128
    length = -(-total // (lanes * groups * 8)) * groups * 8
    flat = jnp.concatenate([part.reshape(-1) for part in parts])
    flat = jnp.pad(flat, (0, length * lanes - total)).reshape(length, lanes)
    for name in SCATTER:
        flat = scatter_sum(flat, name)
    flat = flat.astype(jnp.bfloat16)
    for name in reversed(SCATTER):
        flat = gather_all(flat, name)
    flat = flat.astype(jnp.float32)
    flat = flat.reshape(-1)
    out, start = [], 0
    for part in parts:
        out.append(flat[start : start + part.size].reshape(part.shape))
        start += part.size
    return tuple(out)


def scatter_sum(flat, name):
    count = lax.axis_size(name)
    blocks = flat.astype(jnp.bfloat16).reshape(count, flat.shape[0] // count, flat.shape[1])
    got = lax.all_to_all(blocks, name, 0, 0, tiled=False)
    return jnp.sum(got.astype(jnp.float32), axis=0)


def gather_all(flat, name):
    count = lax.axis_size(name)
    blocks = jnp.broadcast_to(flat[None], (count,) + flat.shape)
    return lax.all_to_all(blocks, name, 0, 0, tiled=False).reshape(-1, flat.shape[1])


def dp_split(mesh):
    column = mesh.devices[:, 0]
    sizes = [len({int(device.coords[axis]) for device in column}) for axis in (1, 0, 2)]
    if math.prod(sizes) != column.size:
        raise ValueError("dp split")
    return tuple(sizes)


def swap_core(value):
    return lax.ppermute(value, "core", [(0, 1), (1, 0)])


def hop(value, source, target):
    return lax.ppermute(value, "zh", [(source, target)])


def keep(valid, new, old):
    return new if old is None else jnp.where(valid, new, old)


def local(latents, clip_of_row, timestep, w_in, w_out, w_mix, w_up, out_grad):
    stages = lax.axis_size("zh")
    stage = lax.axis_index("zh")
    core = lax.axis_index("core")
    first = core == 0
    width = latents.shape[1]
    rows = latents.shape[0] // lax.axis_size("core")

    def pair(weights):
        own = weights[0]
        other = swap_core(own)
        return (jnp.where(first, own, other), jnp.where(first, other, own))

    in_pair, out_pair = pair(w_in), pair(w_out)
    mix_pair, up_pair = pair(w_mix), pair(w_up)

    offset = core * rows
    match = clip_of_row[0][:, None] == jnp.arange(timestep.shape[1], dtype=jnp.int32)[None, :]
    moment = jnp.sum(jnp.where(match, timestep[0][None, :], 0), axis=1).astype(jnp.float32)
    moment = lax.dynamic_slice_in_dim(moment, offset, rows)
    embedding = embed(moment, width)
    source = lax.dynamic_slice_in_dim(latents, offset, rows)
    seed = lax.dynamic_slice_in_dim(out_grad, offset, rows)

    down_in = [None, None]
    skip = [None, None]
    hidden = source
    for tick in range(stages):
        if tick > 0:
            hidden = hop(hidden, tick - 1, tick)
        valid = stage == tick
        lower = hidden
        upper = down_forward(lower, embedding, in_pair[0], out_pair[0])
        hidden = down_forward(upper, embedding, in_pair[1], out_pair[1])
        down_in = [keep(valid, lower, down_in[0]), keep(valid, upper, down_in[1])]
        skip = [keep(valid, upper, skip[0]), keep(valid, hidden, skip[1])]

    up_in = [None, None]
    below = skip[1]
    for tick in range(stages):
        owner = stages - 1 - tick
        if tick > 0:
            below = hop(below, owner + 1, owner)
        valid = stage == owner
        middle = up_forward(below, skip[1], mix_pair[1], up_pair[1])
        up_in = [keep(valid, middle, up_in[0]), keep(valid, below, up_in[1])]
        below = up_forward(middle, skip[0], mix_pair[0], up_pair[0])

    d_skip = [None, None]
    grad_mix = [None, None]
    grad_up = [None, None]
    cotan = seed
    for tick in range(stages):
        if tick > 0:
            cotan = hop(cotan, tick - 1, tick)
        valid = stage == tick
        middle, side0, mix0, up0 = up_backward(up_in[0], skip[0], mix_pair[0], up_pair[0], cotan)
        cotan, side1, mix1, up1 = up_backward(up_in[1], skip[1], mix_pair[1], up_pair[1], middle)
        d_skip = [keep(valid, side0, d_skip[0]), keep(valid, side1, d_skip[1])]
        grad_mix = [keep(valid, mix0, grad_mix[0]), keep(valid, mix1, grad_mix[1])]
        grad_up = [keep(valid, up0, grad_up[0]), keep(valid, up1, grad_up[1])]

    def combine(grads):
        mine = jnp.where(first, grads[0], grads[1])
        theirs = jnp.where(first, grads[1], grads[0])
        return mine + swap_core(theirs)

    factor = 1.0 / math.prod(lax.axis_size(name) for name in DP)

    grad_in = [None, None]
    grad_out = [None, None]
    carry = cotan
    for tick in range(stages):
        owner = stages - 1 - tick
        if tick > 0:
            carry = hop(carry, owner + 1, owner)
        valid = stage == owner
        upper_c = (d_skip[1] + carry.astype(jnp.float32)).astype(jnp.bfloat16)
        upper_d, in1, out1 = down_backward(down_in[1], embedding, in_pair[1], out_pair[1], upper_c)
        lower_c = (d_skip[0] + upper_d.astype(jnp.float32)).astype(jnp.bfloat16)
        carry, in0, out0 = down_backward(down_in[0], embedding, in_pair[0], out_pair[0], lower_c)
        grad_in = [keep(valid, in0, grad_in[0]), keep(valid, in1, grad_in[1])]
        grad_out = [keep(valid, out0, grad_out[0]), keep(valid, out1, grad_out[1])]

    total_in, total_out, total_mix, total_up = reduce_replicas(
        (combine(grad_in), combine(grad_out), combine(grad_mix), combine(grad_up))
    )
    return (
        (total_in * factor)[None],
        (total_out * factor)[None],
        (total_mix * factor)[None],
        (total_up * factor)[None],
    )


def solution(mesh):
    sizes = dp_split(mesh)
    pipe = mesh.devices.shape[1]
    split = Mesh(mesh.devices.reshape(*sizes, pipe // 2, 2), DP + ("zh", "core"))
    sections = ("zh", "core")
    return jax.shard_map(
        local,
        mesh=split,
        in_specs=(
            P(DP, None),
            P(DP, None),
            P(DP, None),
            P(sections, None, None),
            P(sections, None, None),
            P(sections, None, None),
            P(sections, None, None),
            P(DP, None),
        ),
        out_specs=(
            P(sections, None, None),
            P(sections, None, None),
            P(sections, None, None),
            P(sections, None, None),
        ),
        check_vma=False,
    )
```

```python
import math

import jax
import jax.numpy as jnp
from jax import lax
from jax.sharding import Mesh, PartitionSpec as P

DP = ("y", "x", "zl")
SCATTER = ("x", "y", "zl")


def rows_product(left, right):
    return lax.dot_general(
        left, right, (((0,), (0,)), ((), ())), preferred_element_type=jnp.float32
    )


def times_transposed(left, right):
    return lax.dot_general(
        left, right, (((1,), (1,)), ((), ())), preferred_element_type=jnp.float32
    )


def rms_scale(values):
    return lax.rsqrt(jnp.mean(values * values, axis=-1, keepdims=True) + 1e-05)


def silu_slope(values):
    sigma = jax.nn.sigmoid(values)
    return sigma * (1.0 + values * (1.0 - sigma))


def embed(moment, width):
    half = width // 2
    freq = jnp.exp(-math.log(10000.0) * jnp.arange(half, dtype=jnp.float32) / half)
    angle = moment[:, None] * freq[None, :]
    return jnp.concatenate([jnp.sin(angle), jnp.cos(angle)], axis=-1)


def down_forward(hidden, embedding, in_matrix, out_matrix):
    lifted = hidden.astype(jnp.float32) + embedding
    normed = lifted * rms_scale(lifted)
    inner = jnp.dot(normed.astype(jnp.bfloat16), in_matrix, preferred_element_type=jnp.float32)
    gated = jax.nn.silu(inner).astype(jnp.bfloat16)
    return (lifted + jnp.dot(gated, out_matrix, preferred_element_type=jnp.float32)).astype(
        jnp.bfloat16
    )


def down_backward(hidden, embedding, in_matrix, out_matrix, cotan):
    lifted = hidden.astype(jnp.float32) + embedding
    scale = rms_scale(lifted)
    normed = lifted * scale
    normed_b = normed.astype(jnp.bfloat16)
    inner = jnp.dot(normed_b, in_matrix, preferred_element_type=jnp.float32)
    gated = jax.nn.silu(inner).astype(jnp.bfloat16)
    grad_out = rows_product(gated, cotan)
    d_gated = times_transposed(cotan, out_matrix)
    d_inner = (d_gated * silu_slope(inner)).astype(jnp.bfloat16)
    grad_in = rows_product(normed_b, d_inner)
    d_normed = times_transposed(d_inner, in_matrix)
    d_lifted = cotan.astype(jnp.float32) + scale * (
        d_normed - normed * jnp.mean(d_normed * normed, axis=-1, keepdims=True)
    )
    return (d_lifted.astype(jnp.bfloat16), grad_in, grad_out)


def up_forward(below, side, mix_matrix, up_matrix):
    joined = jnp.concatenate([below, side], axis=-1)
    mixed = jnp.dot(joined, mix_matrix, preferred_element_type=jnp.float32)
    normed = mixed * rms_scale(mixed)
    active = jax.nn.silu(normed).astype(jnp.bfloat16)
    return (mixed + jnp.dot(active, up_matrix, preferred_element_type=jnp.float32)).astype(
        jnp.bfloat16
    )


def up_backward(below, side, mix_matrix, up_matrix, cotan):
    width = below.shape[-1]
    joined = jnp.concatenate([below, side], axis=-1)
    mixed = jnp.dot(joined, mix_matrix, preferred_element_type=jnp.float32)
    scale = rms_scale(mixed)
    normed = mixed * scale
    active = jax.nn.silu(normed).astype(jnp.bfloat16)
    grad_up = rows_product(active, cotan)
    d_active = times_transposed(cotan, up_matrix)
    d_normed = d_active * silu_slope(normed)
    d_mixed = (
        cotan.astype(jnp.float32)
        + scale * (d_normed - normed * jnp.mean(d_normed * normed, axis=-1, keepdims=True))
    ).astype(jnp.bfloat16)
    grad_mix = rows_product(joined, d_mixed)
    d_joined = times_transposed(d_mixed, mix_matrix)
    return (d_joined[:, :width].astype(jnp.bfloat16), d_joined[:, width:], grad_mix, grad_up)


def reduce_replicas(parts):
    total = sum(part.size for part in parts)
    groups = math.prod(lax.axis_size(name) for name in DP)
    lanes = 128
    length = -(-total // (lanes * groups * 8)) * groups * 8
    flat = jnp.concatenate([part.reshape(-1) for part in parts])
    flat = jnp.pad(flat, (0, length * lanes - total)).reshape(length, lanes)
    for name in SCATTER:
        flat = scatter_sum(flat, name)
    flat = flat.astype(jnp.bfloat16)
    for name in reversed(SCATTER):
        flat = gather_all(flat, name)
    flat = flat.astype(jnp.float32) * (1.0 / groups)
    flat = flat.reshape(-1)
    out, start = [], 0
    for part in parts:
        out.append(flat[start : start + part.size].reshape(part.shape))
        start += part.size
    return tuple(out)


def scatter_sum(flat, name):
    count = lax.axis_size(name)
    blocks = flat.astype(jnp.bfloat16).reshape(count, flat.shape[0] // count, flat.shape[1])
    got = lax.all_to_all(blocks, name, 0, 0, tiled=False)
    return jnp.sum(got.astype(jnp.float32), axis=0)


def gather_all(flat, name):
    count = lax.axis_size(name)
    blocks = jnp.broadcast_to(flat[None], (count,) + flat.shape)
    return lax.all_to_all(blocks, name, 0, 0, tiled=False).reshape(-1, flat.shape[1])


def dp_split(mesh):
    column = mesh.devices[:, 0]
    sizes = [len({int(device.coords[axis]) for device in column}) for axis in (1, 0, 2)]
    if math.prod(sizes) != column.size:
        raise ValueError("dp split")
    return tuple(sizes)


def swap_core(value):
    return lax.ppermute(value, "core", [(0, 1), (1, 0)])


def hop(value, source, target):
    return lax.ppermute(value, "zh", [(source, target)])


def keep(valid, new, old):
    return new if old is None else jnp.where(valid, new, old)


def local(latents, clip_of_row, timestep, w_in, w_out, w_mix, w_up, out_grad):
    stages = lax.axis_size("zh")
    stage = lax.axis_index("zh")
    core = lax.axis_index("core")
    first = core == 0
    width = latents.shape[1]
    rows = latents.shape[0] // lax.axis_size("core")

    def pair(weights):
        own = weights[0]
        other = swap_core(own)
        return (jnp.where(first, own, other), jnp.where(first, other, own))

    in_pair, out_pair = pair(w_in), pair(w_out)
    mix_pair, up_pair = pair(w_mix), pair(w_up)

    offset = core * rows
    match = clip_of_row[0][:, None] == jnp.arange(timestep.shape[1], dtype=jnp.int32)[None, :]
    moment = jnp.sum(jnp.where(match, timestep[0][None, :], 0), axis=1).astype(jnp.float32)
    moment = lax.dynamic_slice_in_dim(moment, offset, rows)
    embedding = embed(moment, width)
    source = lax.dynamic_slice_in_dim(latents, offset, rows)
    seed = lax.dynamic_slice_in_dim(out_grad, offset, rows)

    down_in = [None, None]
    skip = [None, None]
    hidden = source
    for tick in range(stages):
        if tick > 0:
            hidden = hop(hidden, tick - 1, tick)
        valid = stage == tick
        lower = hidden
        upper = down_forward(lower, embedding, in_pair[0], out_pair[0])
        hidden = down_forward(upper, embedding, in_pair[1], out_pair[1])
        down_in = [keep(valid, lower, down_in[0]), keep(valid, upper, down_in[1])]
        skip = [keep(valid, upper, skip[0]), keep(valid, hidden, skip[1])]

    up_in = [None, None]
    below = skip[1]
    for tick in range(stages):
        owner = stages - 1 - tick
        if tick > 0:
            below = hop(below, owner + 1, owner)
        valid = stage == owner
        middle = up_forward(below, skip[1], mix_pair[1], up_pair[1])
        up_in = [keep(valid, middle, up_in[0]), keep(valid, below, up_in[1])]
        below = up_forward(middle, skip[0], mix_pair[0], up_pair[0])

    d_skip = [None, None]
    grad_mix = [None, None]
    grad_up = [None, None]
    cotan = seed
    for tick in range(stages):
        if tick > 0:
            cotan = hop(cotan, tick - 1, tick)
        valid = stage == tick
        middle, side0, mix0, up0 = up_backward(up_in[0], skip[0], mix_pair[0], up_pair[0], cotan)
        cotan, side1, mix1, up1 = up_backward(up_in[1], skip[1], mix_pair[1], up_pair[1], middle)
        d_skip = [keep(valid, side0, d_skip[0]), keep(valid, side1, d_skip[1])]
        grad_mix = [keep(valid, mix0, grad_mix[0]), keep(valid, mix1, grad_mix[1])]
        grad_up = [keep(valid, up0, grad_up[0]), keep(valid, up1, grad_up[1])]

    def combine(grads):
        mine = jnp.where(first, grads[0], grads[1])
        theirs = jnp.where(first, grads[1], grads[0])
        return mine + swap_core(theirs.astype(jnp.bfloat16)).astype(jnp.float32)


    grad_in = [None, None]
    grad_out = [None, None]
    carry = cotan
    for tick in range(stages):
        owner = stages - 1 - tick
        if tick > 0:
            carry = hop(carry, owner + 1, owner)
        valid = stage == owner
        upper_c = (d_skip[1] + carry.astype(jnp.float32)).astype(jnp.bfloat16)
        upper_d, in1, out1 = down_backward(down_in[1], embedding, in_pair[1], out_pair[1], upper_c)
        lower_c = (d_skip[0] + upper_d.astype(jnp.float32)).astype(jnp.bfloat16)
        carry, in0, out0 = down_backward(down_in[0], embedding, in_pair[0], out_pair[0], lower_c)
        grad_in = [keep(valid, in0, grad_in[0]), keep(valid, in1, grad_in[1])]
        grad_out = [keep(valid, out0, grad_out[0]), keep(valid, out1, grad_out[1])]

    total_in, total_out, total_mix, total_up = reduce_replicas(
        (combine(grad_in), combine(grad_out), combine(grad_mix), combine(grad_up))
    )
    return (total_in[None], total_out[None], total_mix[None], total_up[None])


def solution(mesh):
    sizes = dp_split(mesh)
    pipe = mesh.devices.shape[1]
    split = Mesh(mesh.devices.reshape(*sizes, pipe // 2, 2), DP + ("zh", "core"))
    sections = ("zh", "core")
    return jax.shard_map(
        local,
        mesh=split,
        in_specs=(
            P(DP, None),
            P(DP, None),
            P(DP, None),
            P(sections, None, None),
            P(sections, None, None),
            P(sections, None, None),
            P(sections, None, None),
            P(DP, None),
        ),
        out_specs=(
            P(sections, None, None),
            P(sections, None, None),
            P(sections, None, None),
            P(sections, None, None),
        ),
        check_vma=False,
    )
```

```python
import math

import jax
import jax.numpy as jnp
from jax import lax
from jax.sharding import Mesh, PartitionSpec as P

DP = ("y", "x", "zl")
SCATTER = ("x", ("y", "zl"))


def rows_product(left, right):
    return lax.dot_general(
        left, right, (((0,), (0,)), ((), ())), preferred_element_type=jnp.float32
    )


def times_transposed(left, right):
    return lax.dot_general(
        left, right, (((1,), (1,)), ((), ())), preferred_element_type=jnp.float32
    )


def rms_scale(values):
    return lax.rsqrt(jnp.mean(values * values, axis=-1, keepdims=True) + 1e-05)


def silu_slope(values):
    sigma = jax.nn.sigmoid(values)
    return sigma * (1.0 + values * (1.0 - sigma))


def embed(moment, width):
    half = width // 2
    freq = jnp.exp(-math.log(10000.0) * jnp.arange(half, dtype=jnp.float32) / half)
    angle = moment[:, None] * freq[None, :]
    return jnp.concatenate([jnp.sin(angle), jnp.cos(angle)], axis=-1)


def down_forward(hidden, embedding, in_matrix, out_matrix):
    lifted = hidden.astype(jnp.float32) + embedding
    normed = lifted * rms_scale(lifted)
    inner = jnp.dot(normed.astype(jnp.bfloat16), in_matrix, preferred_element_type=jnp.float32)
    gated = jax.nn.silu(inner).astype(jnp.bfloat16)
    return (lifted + jnp.dot(gated, out_matrix, preferred_element_type=jnp.float32)).astype(
        jnp.bfloat16
    )


def down_backward(hidden, embedding, in_matrix, out_matrix, cotan):
    lifted = hidden.astype(jnp.float32) + embedding
    scale = rms_scale(lifted)
    normed = lifted * scale
    normed_b = normed.astype(jnp.bfloat16)
    inner = jnp.dot(normed_b, in_matrix, preferred_element_type=jnp.float32)
    gated = jax.nn.silu(inner).astype(jnp.bfloat16)
    grad_out = rows_product(gated, cotan)
    d_gated = times_transposed(cotan, out_matrix)
    d_inner = (d_gated * silu_slope(inner)).astype(jnp.bfloat16)
    grad_in = rows_product(normed_b, d_inner)
    d_normed = times_transposed(d_inner, in_matrix)
    d_lifted = cotan.astype(jnp.float32) + scale * (
        d_normed - normed * jnp.mean(d_normed * normed, axis=-1, keepdims=True)
    )
    return (d_lifted.astype(jnp.bfloat16), grad_in, grad_out)


def up_forward(below, side, mix_matrix, up_matrix):
    joined = jnp.concatenate([below, side], axis=-1)
    mixed = jnp.dot(joined, mix_matrix, preferred_element_type=jnp.float32)
    normed = mixed * rms_scale(mixed)
    active = jax.nn.silu(normed).astype(jnp.bfloat16)
    return (mixed + jnp.dot(active, up_matrix, preferred_element_type=jnp.float32)).astype(
        jnp.bfloat16
    )


def up_backward(below, side, mix_matrix, up_matrix, cotan):
    width = below.shape[-1]
    joined = jnp.concatenate([below, side], axis=-1)
    mixed = jnp.dot(joined, mix_matrix, preferred_element_type=jnp.float32)
    scale = rms_scale(mixed)
    normed = mixed * scale
    active = jax.nn.silu(normed).astype(jnp.bfloat16)
    grad_up = rows_product(active, cotan)
    d_active = times_transposed(cotan, up_matrix)
    d_normed = d_active * silu_slope(normed)
    d_mixed = (
        cotan.astype(jnp.float32)
        + scale * (d_normed - normed * jnp.mean(d_normed * normed, axis=-1, keepdims=True))
    ).astype(jnp.bfloat16)
    grad_mix = rows_product(joined, d_mixed)
    d_joined = times_transposed(d_mixed, mix_matrix)
    return (d_joined[:, :width].astype(jnp.bfloat16), d_joined[:, width:], grad_mix, grad_up)


def reduce_replicas(parts):
    total = sum(part.size for part in parts)
    groups = math.prod(lax.axis_size(name) for name in DP)
    lanes = 128
    length = -(-total // (lanes * groups * 8)) * groups * 8
    flat = jnp.concatenate([part.reshape(-1) for part in parts])
    flat = jnp.pad(flat, (0, length * lanes - total)).reshape(length, lanes)
    for name in SCATTER:
        flat = scatter_sum(flat, name)
    flat = flat.astype(jnp.bfloat16)
    for name in reversed(SCATTER):
        flat = gather_all(flat, name)
    flat = flat.astype(jnp.float32) * (1.0 / groups)
    flat = flat.reshape(-1)
    out, start = [], 0
    for part in parts:
        out.append(flat[start : start + part.size].reshape(part.shape))
        start += part.size
    return tuple(out)


def axis_count(name):
    return math.prod(lax.axis_size(part) for part in (name if isinstance(name, tuple) else (name,)))


def scatter_sum(flat, name):
    count = axis_count(name)
    blocks = flat.astype(jnp.bfloat16).reshape(count, flat.shape[0] // count, flat.shape[1])
    got = lax.all_to_all(blocks, name, 0, 0, tiled=False)
    return jnp.sum(got.astype(jnp.float32), axis=0)


def gather_all(flat, name):
    count = axis_count(name)
    blocks = jnp.broadcast_to(flat[None], (count,) + flat.shape)
    return lax.all_to_all(blocks, name, 0, 0, tiled=False).reshape(-1, flat.shape[1])


def dp_split(mesh):
    column = mesh.devices[:, 0]
    sizes = [len({int(device.coords[axis]) for device in column}) for axis in (1, 0, 2)]
    if math.prod(sizes) != column.size:
        raise ValueError("dp split")
    return tuple(sizes)


def swap_core(value):
    return lax.ppermute(value, "core", [(0, 1), (1, 0)])


def hop(value, source, target):
    return lax.ppermute(value, "zh", [(source, target)])


def keep(valid, new, old):
    return new if old is None else jnp.where(valid, new, old)


def local(latents, clip_of_row, timestep, w_in, w_out, w_mix, w_up, out_grad):
    stages = lax.axis_size("zh")
    stage = lax.axis_index("zh")
    core = lax.axis_index("core")
    first = core == 0
    width = latents.shape[1]
    rows = latents.shape[0] // lax.axis_size("core")

    def pair(weights):
        own = weights[0]
        other = swap_core(own)
        return (jnp.where(first, own, other), jnp.where(first, other, own))

    in_pair, out_pair = pair(w_in), pair(w_out)
    mix_pair, up_pair = pair(w_mix), pair(w_up)

    offset = core * rows
    match = clip_of_row[0][:, None] == jnp.arange(timestep.shape[1], dtype=jnp.int32)[None, :]
    moment = jnp.sum(jnp.where(match, timestep[0][None, :], 0), axis=1).astype(jnp.float32)
    moment = lax.dynamic_slice_in_dim(moment, offset, rows)
    embedding = embed(moment, width)
    source = lax.dynamic_slice_in_dim(latents, offset, rows)
    seed = lax.dynamic_slice_in_dim(out_grad, offset, rows)

    down_in = [None, None]
    skip = [None, None]
    hidden = source
    for tick in range(stages):
        if tick > 0:
            hidden = hop(hidden, tick - 1, tick)
        valid = stage == tick
        lower = hidden
        upper = down_forward(lower, embedding, in_pair[0], out_pair[0])
        hidden = down_forward(upper, embedding, in_pair[1], out_pair[1])
        down_in = [keep(valid, lower, down_in[0]), keep(valid, upper, down_in[1])]
        skip = [keep(valid, upper, skip[0]), keep(valid, hidden, skip[1])]

    up_in = [None, None]
    below = skip[1]
    for tick in range(stages):
        owner = stages - 1 - tick
        if tick > 0:
            below = hop(below, owner + 1, owner)
        valid = stage == owner
        middle = up_forward(below, skip[1], mix_pair[1], up_pair[1])
        up_in = [keep(valid, middle, up_in[0]), keep(valid, below, up_in[1])]
        below = up_forward(middle, skip[0], mix_pair[0], up_pair[0])

    d_skip = [None, None]
    grad_mix = [None, None]
    grad_up = [None, None]
    cotan = seed
    for tick in range(stages):
        if tick > 0:
            cotan = hop(cotan, tick - 1, tick)
        valid = stage == tick
        middle, side0, mix0, up0 = up_backward(up_in[0], skip[0], mix_pair[0], up_pair[0], cotan)
        cotan, side1, mix1, up1 = up_backward(up_in[1], skip[1], mix_pair[1], up_pair[1], middle)
        d_skip = [keep(valid, side0, d_skip[0]), keep(valid, side1, d_skip[1])]
        grad_mix = [keep(valid, mix0, grad_mix[0]), keep(valid, mix1, grad_mix[1])]
        grad_up = [keep(valid, up0, grad_up[0]), keep(valid, up1, grad_up[1])]

    def combine(grads):
        mine = jnp.where(first, grads[0], grads[1])
        theirs = jnp.where(first, grads[1], grads[0])
        return mine + swap_core(theirs.astype(jnp.bfloat16)).astype(jnp.float32)


    grad_in = [None, None]
    grad_out = [None, None]
    carry = cotan
    for tick in range(stages):
        owner = stages - 1 - tick
        if tick > 0:
            carry = hop(carry, owner + 1, owner)
        valid = stage == owner
        upper_c = (d_skip[1] + carry.astype(jnp.float32)).astype(jnp.bfloat16)
        upper_d, in1, out1 = down_backward(down_in[1], embedding, in_pair[1], out_pair[1], upper_c)
        lower_c = (d_skip[0] + upper_d.astype(jnp.float32)).astype(jnp.bfloat16)
        carry, in0, out0 = down_backward(down_in[0], embedding, in_pair[0], out_pair[0], lower_c)
        grad_in = [keep(valid, in0, grad_in[0]), keep(valid, in1, grad_in[1])]
        grad_out = [keep(valid, out0, grad_out[0]), keep(valid, out1, grad_out[1])]

    total_in, total_out, total_mix, total_up = reduce_replicas(
        (combine(grad_in), combine(grad_out), combine(grad_mix), combine(grad_up))
    )
    return (total_in[None], total_out[None], total_mix[None], total_up[None])


def solution(mesh):
    sizes = dp_split(mesh)
    pipe = mesh.devices.shape[1]
    split = Mesh(mesh.devices.reshape(*sizes, pipe // 2, 2), DP + ("zh", "core"))
    sections = ("zh", "core")
    return jax.shard_map(
        local,
        mesh=split,
        in_specs=(
            P(DP, None),
            P(DP, None),
            P(DP, None),
            P(sections, None, None),
            P(sections, None, None),
            P(sections, None, None),
            P(sections, None, None),
            P(DP, None),
        ),
        out_specs=(
            P(sections, None, None),
            P(sections, None, None),
            P(sections, None, None),
            P(sections, None, None),
        ),
        check_vma=False,
    )
```

```python
import math

import jax
import jax.numpy as jnp
from jax import lax
from jax.sharding import Mesh, PartitionSpec as P

DP = ("y", "x", "zl")
SCATTER = ("x", ("y", "zl"))


def rows_product(left, right):
    return lax.dot_general(
        left, right, (((0,), (0,)), ((), ())), preferred_element_type=jnp.float32
    )


def times_transposed(left, right):
    return lax.dot_general(
        left, right, (((1,), (1,)), ((), ())), preferred_element_type=jnp.float32
    )


def rms_scale(values):
    return lax.rsqrt(jnp.mean(values * values, axis=-1, keepdims=True) + 1e-05)


def silu_slope(values):
    sigma = jax.nn.sigmoid(values)
    return sigma * (1.0 + values * (1.0 - sigma))


def embed(moment, width):
    half = width // 2
    freq = jnp.exp(-math.log(10000.0) * jnp.arange(half, dtype=jnp.float32) / half)
    angle = moment[:, None] * freq[None, :]
    return jnp.concatenate([jnp.sin(angle), jnp.cos(angle)], axis=-1)


def down_forward(hidden, embedding, in_matrix, out_matrix):
    lifted = hidden.astype(jnp.float32) + embedding
    normed = lifted * rms_scale(lifted)
    inner = jnp.dot(normed.astype(jnp.bfloat16), in_matrix, preferred_element_type=jnp.float32)
    gated = jax.nn.silu(inner).astype(jnp.bfloat16)
    return (lifted + jnp.dot(gated, out_matrix, preferred_element_type=jnp.float32)).astype(
        jnp.bfloat16
    )


def down_backward(hidden, embedding, in_matrix, out_matrix, cotan):
    lifted = hidden.astype(jnp.float32) + embedding
    scale = rms_scale(lifted)
    normed = lifted * scale
    normed_b = normed.astype(jnp.bfloat16)
    inner = jnp.dot(normed_b, in_matrix, preferred_element_type=jnp.float32)
    gated = jax.nn.silu(inner).astype(jnp.bfloat16)
    grad_out = rows_product(gated, cotan)
    d_gated = times_transposed(cotan, out_matrix)
    d_inner = (d_gated * silu_slope(inner)).astype(jnp.bfloat16)
    grad_in = rows_product(normed_b, d_inner)
    d_normed = times_transposed(d_inner, in_matrix)
    d_lifted = cotan.astype(jnp.float32) + scale * (
        d_normed - normed * jnp.mean(d_normed * normed, axis=-1, keepdims=True)
    )
    return (d_lifted.astype(jnp.bfloat16), grad_in, grad_out)


def up_forward(below, side, mix_matrix, up_matrix):
    joined = jnp.concatenate([below, side], axis=-1)
    mixed = jnp.dot(joined, mix_matrix, preferred_element_type=jnp.float32)
    normed = mixed * rms_scale(mixed)
    active = jax.nn.silu(normed).astype(jnp.bfloat16)
    return (mixed + jnp.dot(active, up_matrix, preferred_element_type=jnp.float32)).astype(
        jnp.bfloat16
    )


def up_backward(below, side, mix_matrix, up_matrix, cotan):
    width = below.shape[-1]
    joined = jnp.concatenate([below, side], axis=-1)
    mixed = jnp.dot(joined, mix_matrix, preferred_element_type=jnp.float32)
    scale = rms_scale(mixed)
    normed = mixed * scale
    active = jax.nn.silu(normed).astype(jnp.bfloat16)
    grad_up = rows_product(active, cotan)
    d_active = times_transposed(cotan, up_matrix)
    d_normed = d_active * silu_slope(normed)
    d_mixed = (
        cotan.astype(jnp.float32)
        + scale * (d_normed - normed * jnp.mean(d_normed * normed, axis=-1, keepdims=True))
    ).astype(jnp.bfloat16)
    grad_mix = rows_product(joined, d_mixed)
    d_joined = times_transposed(d_mixed, mix_matrix)
    return (d_joined[:, :width].astype(jnp.bfloat16), d_joined[:, width:], grad_mix, grad_up)


def reduce_replicas(parts, tail, tail_shapes):
    shapes = [part.shape for part in parts] + list(tail_shapes)
    total = sum(math.prod(shape) for shape in shapes)
    groups = math.prod(lax.axis_size(name) for name in DP)
    lanes = 128
    length = -(-total // (lanes * groups * 8)) * groups * 8
    flat = jnp.concatenate([part.reshape(-1) for part in parts] + [tail])
    flat = jnp.pad(flat, (0, length * lanes - total)).reshape(length, lanes)
    for name in SCATTER:
        flat = scatter_sum(flat, name)
    flat = flat.astype(jnp.bfloat16)
    for name in reversed(SCATTER):
        flat = gather_all(flat, name)
    flat = flat.astype(jnp.float32) * (1.0 / groups)
    flat = flat.reshape(-1)
    out, start = [], 0
    for shape in shapes:
        out.append(flat[start : start + math.prod(shape)].reshape(shape))
        start += math.prod(shape)
    return tuple(out)


def axis_count(name):
    return math.prod(lax.axis_size(part) for part in (name if isinstance(name, tuple) else (name,)))


def scatter_sum(flat, name):
    count = axis_count(name)
    blocks = flat.astype(jnp.bfloat16).reshape(count, flat.shape[0] // count, flat.shape[1])
    got = lax.all_to_all(blocks, name, 0, 0, tiled=False)
    return jnp.sum(got.astype(jnp.float32), axis=0)


def gather_all(flat, name):
    count = axis_count(name)
    blocks = jnp.broadcast_to(flat[None], (count,) + flat.shape)
    return lax.all_to_all(blocks, name, 0, 0, tiled=False).reshape(-1, flat.shape[1])


def dp_split(mesh):
    column = mesh.devices[:, 0]
    sizes = [len({int(device.coords[axis]) for device in column}) for axis in (1, 0, 2)]
    if math.prod(sizes) != column.size:
        raise ValueError("dp split")
    return tuple(sizes)


def swap_core(value):
    return lax.ppermute(value, "core", [(0, 1), (1, 0)])


def hop(value, source, target):
    return lax.ppermute(value, "zh", [(source, target)])


def keep(valid, new, old):
    return new if old is None else jnp.where(valid, new, old)


def local(latents, clip_of_row, timestep, w_in, w_out, w_mix, w_up, out_grad):
    stages = lax.axis_size("zh")
    stage = lax.axis_index("zh")
    core = lax.axis_index("core")
    first = core == 0
    width = latents.shape[1]
    rows = latents.shape[0] // lax.axis_size("core")

    def pair(weights):
        own = weights[0]
        other = swap_core(own)
        return (jnp.where(first, own, other), jnp.where(first, other, own))

    in_pair, out_pair = pair(w_in), pair(w_out)

    offset = core * rows
    match = clip_of_row[0][:, None] == jnp.arange(timestep.shape[1], dtype=jnp.int32)[None, :]
    moment = jnp.sum(jnp.where(match, timestep[0][None, :], 0), axis=1).astype(jnp.float32)
    moment = lax.dynamic_slice_in_dim(moment, offset, rows)
    embedding = embed(moment, width)
    source = lax.dynamic_slice_in_dim(latents, offset, rows)
    seed = lax.dynamic_slice_in_dim(out_grad, offset, rows)

    down_in = [None, None]
    skip = [None, None]
    hidden = source
    for tick in range(stages):
        if tick > 0:
            hidden = hop(hidden, tick - 1, tick)
        valid = stage == tick
        lower = hidden
        upper = down_forward(lower, embedding, in_pair[0], out_pair[0])
        hidden = down_forward(upper, embedding, in_pair[1], out_pair[1])
        down_in = [keep(valid, lower, down_in[0]), keep(valid, upper, down_in[1])]
        skip = [keep(valid, upper, skip[0]), keep(valid, hidden, skip[1])]
        if tick == 0:
            w_mix, w_up, hidden = lax.optimization_barrier((w_mix, w_up, hidden))
            mix_pair, up_pair = pair(w_mix), pair(w_up)

    up_in = [None, None]
    below = skip[1]
    for tick in range(stages):
        owner = stages - 1 - tick
        if tick > 0:
            below = hop(below, owner + 1, owner)
        valid = stage == owner
        middle = up_forward(below, skip[1], mix_pair[1], up_pair[1])
        up_in = [keep(valid, middle, up_in[0]), keep(valid, below, up_in[1])]
        below = up_forward(middle, skip[0], mix_pair[0], up_pair[0])

    d_skip = [None, None]
    grad_mix = [None, None]
    grad_up = [None, None]
    cotan = seed
    for tick in range(stages):
        if tick > 0:
            cotan = hop(cotan, tick - 1, tick)
        valid = stage == tick
        middle, side0, mix0, up0 = up_backward(up_in[0], skip[0], mix_pair[0], up_pair[0], cotan)
        cotan, side1, mix1, up1 = up_backward(up_in[1], skip[1], mix_pair[1], up_pair[1], middle)
        d_skip = [keep(valid, side0, d_skip[0]), keep(valid, side1, d_skip[1])]
        grad_mix = [keep(valid, mix0, grad_mix[0]), keep(valid, mix1, grad_mix[1])]
        grad_up = [keep(valid, up0, grad_up[0]), keep(valid, up1, grad_up[1])]

    def combine(grads):
        mine = jnp.where(first, grads[0], grads[1])
        theirs = jnp.where(first, grads[1], grads[0])
        return mine + swap_core(theirs.astype(jnp.bfloat16)).astype(jnp.float32)


    up_flat = jnp.concatenate(
        [combine(grad_mix).reshape(-1), combine(grad_up).reshape(-1)]
    )
    grad_in = [None, None]
    grad_out = [None, None]
    carry = cotan
    for tick in range(stages):
        owner = stages - 1 - tick
        if tick > 0:
            carry = hop(carry, owner + 1, owner)
        if tick == 1:
            carry, up_flat = lax.optimization_barrier((carry, up_flat))
        valid = stage == owner
        upper_c = (d_skip[1] + carry.astype(jnp.float32)).astype(jnp.bfloat16)
        upper_d, in1, out1 = down_backward(down_in[1], embedding, in_pair[1], out_pair[1], upper_c)
        lower_c = (d_skip[0] + upper_d.astype(jnp.float32)).astype(jnp.bfloat16)
        carry, in0, out0 = down_backward(down_in[0], embedding, in_pair[0], out_pair[0], lower_c)
        grad_in = [keep(valid, in0, grad_in[0]), keep(valid, in1, grad_in[1])]
        grad_out = [keep(valid, out0, grad_out[0]), keep(valid, out1, grad_out[1])]

    total_in, total_out, total_mix, total_up = reduce_replicas(
        (combine(grad_in), combine(grad_out)), up_flat, (grad_mix[0].shape, grad_up[0].shape)
    )
    return (total_in[None], total_out[None], total_mix[None], total_up[None])


def solution(mesh):
    sizes = dp_split(mesh)
    pipe = mesh.devices.shape[1]
    split = Mesh(mesh.devices.reshape(*sizes, pipe // 2, 2), DP + ("zh", "core"))
    sections = ("zh", "core")
    return jax.shard_map(
        local,
        mesh=split,
        in_specs=(
            P(DP, None),
            P(DP, None),
            P(DP, None),
            P(sections, None, None),
            P(sections, None, None),
            P(sections, None, None),
            P(sections, None, None),
            P(DP, None),
        ),
        out_specs=(
            P(sections, None, None),
            P(sections, None, None),
            P(sections, None, None),
            P(sections, None, None),
        ),
        check_vma=False,
    )
```

```python
import math

import jax
import jax.numpy as jnp
from jax import lax
from jax.sharding import Mesh, PartitionSpec as P

DP = ("y", "x", "zl")
SCATTER = ("x", ("y", "zl"))


def rows_product(left, right):
    return lax.dot_general(
        left, right, (((0,), (0,)), ((), ())), preferred_element_type=jnp.float32
    )


def times_transposed(left, right):
    return lax.dot_general(
        left, right, (((1,), (1,)), ((), ())), preferred_element_type=jnp.float32
    )


def rms_scale(values):
    return lax.rsqrt(jnp.mean(values * values, axis=-1, keepdims=True) + 1e-05)


def silu_slope(values):
    sigma = jax.nn.sigmoid(values)
    return sigma * (1.0 + values * (1.0 - sigma))


def embed(moment, width):
    half = width // 2
    freq = jnp.exp(-math.log(10000.0) * jnp.arange(half, dtype=jnp.float32) / half)
    angle = moment[:, None] * freq[None, :]
    return jnp.concatenate([jnp.sin(angle), jnp.cos(angle)], axis=-1)


def down_forward(hidden, embedding, in_matrix, out_matrix):
    lifted = hidden.astype(jnp.float32) + embedding
    normed = lifted * rms_scale(lifted)
    inner = jnp.dot(normed.astype(jnp.bfloat16), in_matrix, preferred_element_type=jnp.float32)
    gated = jax.nn.silu(inner).astype(jnp.bfloat16)
    return (lifted + jnp.dot(gated, out_matrix, preferred_element_type=jnp.float32)).astype(
        jnp.bfloat16
    )


def down_backward(hidden, embedding, in_matrix, out_matrix, cotan):
    lifted = hidden.astype(jnp.float32) + embedding
    scale = rms_scale(lifted)
    normed = lifted * scale
    normed_b = normed.astype(jnp.bfloat16)
    inner = jnp.dot(normed_b, in_matrix, preferred_element_type=jnp.float32)
    gated = jax.nn.silu(inner).astype(jnp.bfloat16)
    grad_out = rows_product(gated, cotan)
    d_gated = times_transposed(cotan, out_matrix)
    d_inner = (d_gated * silu_slope(inner)).astype(jnp.bfloat16)
    grad_in = rows_product(normed_b, d_inner)
    d_normed = times_transposed(d_inner, in_matrix)
    d_lifted = cotan.astype(jnp.float32) + scale * (
        d_normed - normed * jnp.mean(d_normed * normed, axis=-1, keepdims=True)
    )
    return (d_lifted.astype(jnp.bfloat16), grad_in, grad_out)


def up_forward(below, side, mix_matrix, up_matrix):
    joined = jnp.concatenate([below, side], axis=-1)
    mixed = jnp.dot(joined, mix_matrix, preferred_element_type=jnp.float32)
    normed = mixed * rms_scale(mixed)
    active = jax.nn.silu(normed).astype(jnp.bfloat16)
    return (mixed + jnp.dot(active, up_matrix, preferred_element_type=jnp.float32)).astype(
        jnp.bfloat16
    )


def up_backward(below, side, mix_matrix, up_matrix, cotan):
    width = below.shape[-1]
    joined = jnp.concatenate([below, side], axis=-1)
    mixed = jnp.dot(joined, mix_matrix, preferred_element_type=jnp.float32)
    scale = rms_scale(mixed)
    normed = mixed * scale
    active = jax.nn.silu(normed).astype(jnp.bfloat16)
    grad_up = rows_product(active, cotan)
    d_active = times_transposed(cotan, up_matrix)
    d_normed = d_active * silu_slope(normed)
    d_mixed = (
        cotan.astype(jnp.float32)
        + scale * (d_normed - normed * jnp.mean(d_normed * normed, axis=-1, keepdims=True))
    ).astype(jnp.bfloat16)
    grad_mix = rows_product(joined, d_mixed)
    d_joined = times_transposed(d_mixed, mix_matrix)
    return (d_joined[:, :width].astype(jnp.bfloat16), d_joined[:, width:], grad_mix, grad_up)


def up_forward_saving(below, side, mix_matrix, up_matrix):
    joined = jnp.concatenate([below, side], axis=-1)
    mixed = jnp.dot(joined, mix_matrix, preferred_element_type=jnp.float32)
    scale = rms_scale(mixed)
    normed = mixed * scale
    active = jax.nn.silu(normed).astype(jnp.bfloat16)
    result = (mixed + jnp.dot(active, up_matrix, preferred_element_type=jnp.float32)).astype(
        jnp.bfloat16
    )
    return result, (joined, scale, normed, active)


def up_backward_saved(saved, mix_matrix, up_matrix, cotan):
    joined, scale, normed, active = saved
    width = joined.shape[-1] // 2
    grad_up = rows_product(active, cotan)
    d_active = times_transposed(cotan, up_matrix)
    d_normed = d_active * silu_slope(normed)
    d_mixed = (
        cotan.astype(jnp.float32)
        + scale * (d_normed - normed * jnp.mean(d_normed * normed, axis=-1, keepdims=True))
    ).astype(jnp.bfloat16)
    grad_mix = rows_product(joined, d_mixed)
    d_joined = times_transposed(d_mixed, mix_matrix)
    return (d_joined[:, :width].astype(jnp.bfloat16), d_joined[:, width:], grad_mix, grad_up)


def keep_all(valid, new, old):
    if old is None:
        return new
    return tuple(jnp.where(valid, a, b) for a, b in zip(new, old))


def reduce_replicas(parts, tail, tail_shapes):
    shapes = [part.shape for part in parts] + list(tail_shapes)
    total = sum(math.prod(shape) for shape in shapes)
    groups = math.prod(lax.axis_size(name) for name in DP)
    lanes = 128
    length = -(-total // (lanes * groups * 8)) * groups * 8
    flat = jnp.concatenate([part.reshape(-1) for part in parts] + [tail])
    flat = jnp.pad(flat, (0, length * lanes - total)).reshape(length, lanes)
    for name in SCATTER:
        flat = scatter_sum(flat, name)
    flat = flat.astype(jnp.bfloat16)
    for name in reversed(SCATTER):
        flat = gather_all(flat, name)
    flat = flat.astype(jnp.float32) * (1.0 / groups)
    flat = flat.reshape(-1)
    out, start = [], 0
    for shape in shapes:
        out.append(flat[start : start + math.prod(shape)].reshape(shape))
        start += math.prod(shape)
    return tuple(out)


def axis_count(name):
    return math.prod(lax.axis_size(part) for part in (name if isinstance(name, tuple) else (name,)))


def scatter_sum(flat, name):
    count = axis_count(name)
    blocks = flat.astype(jnp.bfloat16).reshape(count, flat.shape[0] // count, flat.shape[1])
    got = lax.all_to_all(blocks, name, 0, 0, tiled=False)
    return jnp.sum(got.astype(jnp.float32), axis=0)


def gather_all(flat, name):
    count = axis_count(name)
    blocks = jnp.broadcast_to(flat[None], (count,) + flat.shape)
    return lax.all_to_all(blocks, name, 0, 0, tiled=False).reshape(-1, flat.shape[1])


def dp_split(mesh):
    column = mesh.devices[:, 0]
    sizes = [len({int(device.coords[axis]) for device in column}) for axis in (1, 0, 2)]
    if math.prod(sizes) != column.size:
        raise ValueError("dp split")
    return tuple(sizes)


def swap_core(value):
    return lax.ppermute(value, "core", [(0, 1), (1, 0)])


def hop(value, source, target):
    return lax.ppermute(value, "zh", [(source, target)])


def keep(valid, new, old):
    return new if old is None else jnp.where(valid, new, old)


def local(latents, clip_of_row, timestep, w_in, w_out, w_mix, w_up, out_grad):
    stages = lax.axis_size("zh")
    stage = lax.axis_index("zh")
    core = lax.axis_index("core")
    first = core == 0
    width = latents.shape[1]
    rows = latents.shape[0] // lax.axis_size("core")

    def pair(weights):
        own = weights[0]
        other = swap_core(own)
        return (jnp.where(first, own, other), jnp.where(first, other, own))

    in_pair, out_pair = pair(w_in), pair(w_out)

    offset = core * rows
    match = clip_of_row[0][:, None] == jnp.arange(timestep.shape[1], dtype=jnp.int32)[None, :]
    moment = jnp.sum(jnp.where(match, timestep[0][None, :], 0), axis=1).astype(jnp.float32)
    moment = lax.dynamic_slice_in_dim(moment, offset, rows)
    embedding = embed(moment, width)
    source = lax.dynamic_slice_in_dim(latents, offset, rows)
    seed = lax.dynamic_slice_in_dim(out_grad, offset, rows)

    down_in = [None, None]
    skip = [None, None]
    hidden = source
    for tick in range(stages):
        if tick > 0:
            hidden = hop(hidden, tick - 1, tick)
        valid = stage == tick
        lower = hidden
        upper = down_forward(lower, embedding, in_pair[0], out_pair[0])
        hidden = down_forward(upper, embedding, in_pair[1], out_pair[1])
        down_in = [keep(valid, lower, down_in[0]), keep(valid, upper, down_in[1])]
        skip = [keep(valid, upper, skip[0]), keep(valid, hidden, skip[1])]
        if tick == 0:
            w_mix, w_up, hidden = lax.optimization_barrier((w_mix, w_up, hidden))
            mix_pair, up_pair = pair(w_mix), pair(w_up)

    up_saved = [None, None]
    below = skip[1]
    for tick in range(stages):
        owner = stages - 1 - tick
        if tick > 0:
            below = hop(below, owner + 1, owner)
        valid = stage == owner
        middle, saved1 = up_forward_saving(below, skip[1], mix_pair[1], up_pair[1])
        below, saved0 = up_forward_saving(middle, skip[0], mix_pair[0], up_pair[0])
        up_saved = [keep_all(valid, saved0, up_saved[0]), keep_all(valid, saved1, up_saved[1])]

    d_skip = [None, None]
    grad_mix = [None, None]
    grad_up = [None, None]
    cotan = seed
    for tick in range(stages):
        if tick > 0:
            cotan = hop(cotan, tick - 1, tick)
        valid = stage == tick
        middle, side0, mix0, up0 = up_backward_saved(up_saved[0], mix_pair[0], up_pair[0], cotan)
        cotan, side1, mix1, up1 = up_backward_saved(up_saved[1], mix_pair[1], up_pair[1], middle)
        d_skip = [keep(valid, side0, d_skip[0]), keep(valid, side1, d_skip[1])]
        grad_mix = [keep(valid, mix0, grad_mix[0]), keep(valid, mix1, grad_mix[1])]
        grad_up = [keep(valid, up0, grad_up[0]), keep(valid, up1, grad_up[1])]

    def combine(grads):
        mine = jnp.where(first, grads[0], grads[1])
        theirs = jnp.where(first, grads[1], grads[0])
        return mine + swap_core(theirs.astype(jnp.bfloat16)).astype(jnp.float32)


    up_flat = jnp.concatenate(
        [combine(grad_mix).reshape(-1), combine(grad_up).reshape(-1)]
    )
    grad_in = [None, None]
    grad_out = [None, None]
    carry = cotan
    for tick in range(stages):
        owner = stages - 1 - tick
        if tick > 0:
            carry = hop(carry, owner + 1, owner)
        if tick == 1:
            carry, up_flat = lax.optimization_barrier((carry, up_flat))
        valid = stage == owner
        upper_c = (d_skip[1] + carry.astype(jnp.float32)).astype(jnp.bfloat16)
        upper_d, in1, out1 = down_backward(down_in[1], embedding, in_pair[1], out_pair[1], upper_c)
        lower_c = (d_skip[0] + upper_d.astype(jnp.float32)).astype(jnp.bfloat16)
        carry, in0, out0 = down_backward(down_in[0], embedding, in_pair[0], out_pair[0], lower_c)
        grad_in = [keep(valid, in0, grad_in[0]), keep(valid, in1, grad_in[1])]
        grad_out = [keep(valid, out0, grad_out[0]), keep(valid, out1, grad_out[1])]

    total_in, total_out, total_mix, total_up = reduce_replicas(
        (combine(grad_in), combine(grad_out)), up_flat, (grad_mix[0].shape, grad_up[0].shape)
    )
    return (total_in[None], total_out[None], total_mix[None], total_up[None])


def solution(mesh):
    sizes = dp_split(mesh)
    pipe = mesh.devices.shape[1]
    split = Mesh(mesh.devices.reshape(*sizes, pipe // 2, 2), DP + ("zh", "core"))
    sections = ("zh", "core")
    return jax.shard_map(
        local,
        mesh=split,
        in_specs=(
            P(DP, None),
            P(DP, None),
            P(DP, None),
            P(sections, None, None),
            P(sections, None, None),
            P(sections, None, None),
            P(sections, None, None),
            P(DP, None),
        ),
        out_specs=(
            P(sections, None, None),
            P(sections, None, None),
            P(sections, None, None),
            P(sections, None, None),
        ),
        check_vma=False,
    )
```

```python
import math

import jax
import jax.numpy as jnp
from jax import lax
from jax.sharding import Mesh, PartitionSpec as P

DP = ("y", "x", "zl")
SCATTER = ("x", ("y", "zl"))


def rows_product(left, right):
    return lax.dot_general(
        left, right, (((0,), (0,)), ((), ())), preferred_element_type=jnp.float32
    )


def times_transposed(left, right):
    return lax.dot_general(
        left, right, (((1,), (1,)), ((), ())), preferred_element_type=jnp.float32
    )


def rms_scale(values):
    return lax.rsqrt(jnp.mean(values * values, axis=-1, keepdims=True) + 1e-05)


def silu_slope(values):
    sigma = jax.nn.sigmoid(values)
    return sigma * (1.0 + values * (1.0 - sigma))


def embed(moment, width):
    half = width // 2
    freq = jnp.exp(-math.log(10000.0) * jnp.arange(half, dtype=jnp.float32) / half)
    angle = moment[:, None] * freq[None, :]
    return jnp.concatenate([jnp.sin(angle), jnp.cos(angle)], axis=-1)


def down_forward(hidden, embedding, in_matrix, out_matrix):
    lifted = hidden.astype(jnp.float32) + embedding
    normed = lifted * rms_scale(lifted)
    inner = jnp.dot(normed.astype(jnp.bfloat16), in_matrix, preferred_element_type=jnp.float32)
    gated = jax.nn.silu(inner).astype(jnp.bfloat16)
    return (lifted + jnp.dot(gated, out_matrix, preferred_element_type=jnp.float32)).astype(
        jnp.bfloat16
    )


def down_backward(hidden, embedding, in_matrix, out_matrix, cotan):
    lifted = hidden.astype(jnp.float32) + embedding
    scale = rms_scale(lifted)
    normed = lifted * scale
    normed_b = normed.astype(jnp.bfloat16)
    inner = jnp.dot(normed_b, in_matrix, preferred_element_type=jnp.float32)
    gated = jax.nn.silu(inner).astype(jnp.bfloat16)
    grad_out = rows_product(gated, cotan)
    d_gated = times_transposed(cotan, out_matrix)
    d_inner = (d_gated * silu_slope(inner)).astype(jnp.bfloat16)
    grad_in = rows_product(normed_b, d_inner)
    d_normed = times_transposed(d_inner, in_matrix)
    d_lifted = cotan.astype(jnp.float32) + scale * (
        d_normed - normed * jnp.mean(d_normed * normed, axis=-1, keepdims=True)
    )
    return (d_lifted.astype(jnp.bfloat16), grad_in, grad_out)


def up_forward(below, side, mix_matrix, up_matrix):
    joined = jnp.concatenate([below, side], axis=-1)
    mixed = jnp.dot(joined, mix_matrix, preferred_element_type=jnp.float32)
    normed = mixed * rms_scale(mixed)
    active = jax.nn.silu(normed).astype(jnp.bfloat16)
    return (mixed + jnp.dot(active, up_matrix, preferred_element_type=jnp.float32)).astype(
        jnp.bfloat16
    )


def up_backward(below, side, mix_matrix, up_matrix, cotan):
    width = below.shape[-1]
    joined = jnp.concatenate([below, side], axis=-1)
    mixed = jnp.dot(joined, mix_matrix, preferred_element_type=jnp.float32)
    scale = rms_scale(mixed)
    normed = mixed * scale
    active = jax.nn.silu(normed).astype(jnp.bfloat16)
    grad_up = rows_product(active, cotan)
    d_active = times_transposed(cotan, up_matrix)
    d_normed = d_active * silu_slope(normed)
    d_mixed = (
        cotan.astype(jnp.float32)
        + scale * (d_normed - normed * jnp.mean(d_normed * normed, axis=-1, keepdims=True))
    ).astype(jnp.bfloat16)
    grad_mix = rows_product(joined, d_mixed)
    d_joined = times_transposed(d_mixed, mix_matrix)
    return (d_joined[:, :width].astype(jnp.bfloat16), d_joined[:, width:], grad_mix, grad_up)


def down_forward_saving(hidden, embedding, in_matrix, out_matrix):
    lifted = hidden.astype(jnp.float32) + embedding
    scale = rms_scale(lifted)
    normed = lifted * scale
    inner = jnp.dot(normed.astype(jnp.bfloat16), in_matrix, preferred_element_type=jnp.float32)
    gated = jax.nn.silu(inner).astype(jnp.bfloat16)
    result = (lifted + jnp.dot(gated, out_matrix, preferred_element_type=jnp.float32)).astype(
        jnp.bfloat16
    )
    return result, (scale, normed)


def down_backward_saved(saved, in_matrix, out_matrix, cotan):
    scale, normed = saved
    normed_b = normed.astype(jnp.bfloat16)
    inner = jnp.dot(normed_b, in_matrix, preferred_element_type=jnp.float32)
    gated = jax.nn.silu(inner).astype(jnp.bfloat16)
    grad_out = rows_product(gated, cotan)
    d_gated = times_transposed(cotan, out_matrix)
    d_inner = (d_gated * silu_slope(inner)).astype(jnp.bfloat16)
    grad_in = rows_product(normed_b, d_inner)
    d_normed = times_transposed(d_inner, in_matrix)
    d_lifted = cotan.astype(jnp.float32) + scale * (
        d_normed - normed * jnp.mean(d_normed * normed, axis=-1, keepdims=True)
    )
    return (d_lifted.astype(jnp.bfloat16), grad_in, grad_out)


def up_forward_saving(below, side, mix_matrix, up_matrix):
    joined = jnp.concatenate([below, side], axis=-1)
    mixed = jnp.dot(joined, mix_matrix, preferred_element_type=jnp.float32)
    scale = rms_scale(mixed)
    normed = mixed * scale
    active = jax.nn.silu(normed).astype(jnp.bfloat16)
    result = (mixed + jnp.dot(active, up_matrix, preferred_element_type=jnp.float32)).astype(
        jnp.bfloat16
    )
    return result, (joined, scale, normed, active)


def up_backward_saved(saved, mix_matrix, up_matrix, cotan):
    joined, scale, normed, active = saved
    width = joined.shape[-1] // 2
    grad_up = rows_product(active, cotan)
    d_active = times_transposed(cotan, up_matrix)
    d_normed = d_active * silu_slope(normed)
    d_mixed = (
        cotan.astype(jnp.float32)
        + scale * (d_normed - normed * jnp.mean(d_normed * normed, axis=-1, keepdims=True))
    ).astype(jnp.bfloat16)
    grad_mix = rows_product(joined, d_mixed)
    d_joined = times_transposed(d_mixed, mix_matrix)
    return (d_joined[:, :width].astype(jnp.bfloat16), d_joined[:, width:], grad_mix, grad_up)


def keep_all(valid, new, old):
    if old is None:
        return new
    return tuple(jnp.where(valid, a, b) for a, b in zip(new, old))


def reduce_replicas(parts, tail, tail_shapes):
    shapes = [part.shape for part in parts] + list(tail_shapes)
    total = sum(math.prod(shape) for shape in shapes)
    groups = math.prod(lax.axis_size(name) for name in DP)
    lanes = 128
    length = -(-total // (lanes * groups * 8)) * groups * 8
    flat = jnp.concatenate([part.reshape(-1) for part in parts] + [tail])
    flat = jnp.pad(flat, (0, length * lanes - total)).reshape(length, lanes)
    for name in SCATTER:
        flat = scatter_sum(flat, name)
    flat = flat.astype(jnp.bfloat16)
    for name in reversed(SCATTER):
        flat = gather_all(flat, name)
    flat = flat.astype(jnp.float32) * (1.0 / groups)
    flat = flat.reshape(-1)
    out, start = [], 0
    for shape in shapes:
        out.append(flat[start : start + math.prod(shape)].reshape(shape))
        start += math.prod(shape)
    return tuple(out)


def axis_count(name):
    return math.prod(lax.axis_size(part) for part in (name if isinstance(name, tuple) else (name,)))


def scatter_sum(flat, name):
    count = axis_count(name)
    blocks = flat.astype(jnp.bfloat16).reshape(count, flat.shape[0] // count, flat.shape[1])
    got = lax.all_to_all(blocks, name, 0, 0, tiled=False)
    return jnp.sum(got.astype(jnp.float32), axis=0)


def gather_all(flat, name):
    count = axis_count(name)
    blocks = jnp.broadcast_to(flat[None], (count,) + flat.shape)
    return lax.all_to_all(blocks, name, 0, 0, tiled=False).reshape(-1, flat.shape[1])


def dp_split(mesh):
    column = mesh.devices[:, 0]
    sizes = [len({int(device.coords[axis]) for device in column}) for axis in (1, 0, 2)]
    if math.prod(sizes) != column.size:
        raise ValueError("dp split")
    return tuple(sizes)


def swap_core(value):
    return lax.ppermute(value, "core", [(0, 1), (1, 0)])


def hop(value, source, target):
    return lax.ppermute(value, "zh", [(source, target)])


def keep(valid, new, old):
    return new if old is None else jnp.where(valid, new, old)


def local(latents, clip_of_row, timestep, w_in, w_out, w_mix, w_up, out_grad):
    stages = lax.axis_size("zh")
    stage = lax.axis_index("zh")
    core = lax.axis_index("core")
    first = core == 0
    width = latents.shape[1]
    rows = latents.shape[0] // lax.axis_size("core")

    def pair(weights):
        own = weights[0]
        other = swap_core(own)
        return (jnp.where(first, own, other), jnp.where(first, other, own))

    in_pair, out_pair = pair(w_in), pair(w_out)

    offset = core * rows
    match = clip_of_row[0][:, None] == jnp.arange(timestep.shape[1], dtype=jnp.int32)[None, :]
    moment = jnp.sum(jnp.where(match, timestep[0][None, :], 0), axis=1).astype(jnp.float32)
    moment = lax.dynamic_slice_in_dim(moment, offset, rows)
    embedding = embed(moment, width)
    source = lax.dynamic_slice_in_dim(latents, offset, rows)
    seed = lax.dynamic_slice_in_dim(out_grad, offset, rows)

    down_saved = [None, None]
    skip = [None, None]
    hidden = source
    for tick in range(stages):
        if tick > 0:
            hidden = hop(hidden, tick - 1, tick)
        valid = stage == tick
        upper, saved0 = down_forward_saving(hidden, embedding, in_pair[0], out_pair[0])
        hidden, saved1 = down_forward_saving(upper, embedding, in_pair[1], out_pair[1])
        down_saved = [keep_all(valid, saved0, down_saved[0]), keep_all(valid, saved1, down_saved[1])]
        skip = [keep(valid, upper, skip[0]), keep(valid, hidden, skip[1])]
        if tick == 0:
            w_mix, w_up, hidden = lax.optimization_barrier((w_mix, w_up, hidden))
            mix_pair, up_pair = pair(w_mix), pair(w_up)

    up_saved = [None, None]
    below = skip[1]
    for tick in range(stages):
        owner = stages - 1 - tick
        if tick > 0:
            below = hop(below, owner + 1, owner)
        valid = stage == owner
        middle, saved1 = up_forward_saving(below, skip[1], mix_pair[1], up_pair[1])
        below, saved0 = up_forward_saving(middle, skip[0], mix_pair[0], up_pair[0])
        up_saved = [keep_all(valid, saved0, up_saved[0]), keep_all(valid, saved1, up_saved[1])]

    d_skip = [None, None]
    grad_mix = [None, None]
    grad_up = [None, None]
    cotan = seed
    for tick in range(stages):
        if tick > 0:
            cotan = hop(cotan, tick - 1, tick)
        valid = stage == tick
        middle, side0, mix0, up0 = up_backward_saved(up_saved[0], mix_pair[0], up_pair[0], cotan)
        cotan, side1, mix1, up1 = up_backward_saved(up_saved[1], mix_pair[1], up_pair[1], middle)
        d_skip = [keep(valid, side0, d_skip[0]), keep(valid, side1, d_skip[1])]
        grad_mix = [keep(valid, mix0, grad_mix[0]), keep(valid, mix1, grad_mix[1])]
        grad_up = [keep(valid, up0, grad_up[0]), keep(valid, up1, grad_up[1])]

    def combine(grads):
        mine = jnp.where(first, grads[0], grads[1])
        theirs = jnp.where(first, grads[1], grads[0])
        return mine + swap_core(theirs.astype(jnp.bfloat16)).astype(jnp.float32)


    up_flat = jnp.concatenate(
        [combine(grad_mix).reshape(-1), combine(grad_up).reshape(-1)]
    )
    grad_in = [None, None]
    grad_out = [None, None]
    carry = cotan
    for tick in range(stages):
        owner = stages - 1 - tick
        if tick > 0:
            carry = hop(carry, owner + 1, owner)
        if tick == 1:
            carry, up_flat = lax.optimization_barrier((carry, up_flat))
        valid = stage == owner
        upper_c = (d_skip[1] + carry.astype(jnp.float32)).astype(jnp.bfloat16)
        upper_d, in1, out1 = down_backward_saved(down_saved[1], in_pair[1], out_pair[1], upper_c)
        lower_c = (d_skip[0] + upper_d.astype(jnp.float32)).astype(jnp.bfloat16)
        carry, in0, out0 = down_backward_saved(down_saved[0], in_pair[0], out_pair[0], lower_c)
        grad_in = [keep(valid, in0, grad_in[0]), keep(valid, in1, grad_in[1])]
        grad_out = [keep(valid, out0, grad_out[0]), keep(valid, out1, grad_out[1])]

    total_in, total_out, total_mix, total_up = reduce_replicas(
        (combine(grad_in), combine(grad_out)), up_flat, (grad_mix[0].shape, grad_up[0].shape)
    )
    return (total_in[None], total_out[None], total_mix[None], total_up[None])


def solution(mesh):
    sizes = dp_split(mesh)
    pipe = mesh.devices.shape[1]
    split = Mesh(mesh.devices.reshape(*sizes, pipe // 2, 2), DP + ("zh", "core"))
    sections = ("zh", "core")
    return jax.shard_map(
        local,
        mesh=split,
        in_specs=(
            P(DP, None),
            P(DP, None),
            P(DP, None),
            P(sections, None, None),
            P(sections, None, None),
            P(sections, None, None),
            P(sections, None, None),
            P(DP, None),
        ),
        out_specs=(
            P(sections, None, None),
            P(sections, None, None),
            P(sections, None, None),
            P(sections, None, None),
        ),
        check_vma=False,
    )
```

```python
import math

import jax
import jax.numpy as jnp
from jax import lax
from jax.sharding import Mesh, PartitionSpec as P

DP = ("y", "x", "zl")
SCATTER = ("x", ("y", "zl"))


def rows_product(left, right):
    return lax.dot_general(
        left, right, (((0,), (0,)), ((), ())), preferred_element_type=jnp.float32
    )


def times_transposed(left, right):
    return lax.dot_general(
        left, right, (((1,), (1,)), ((), ())), preferred_element_type=jnp.float32
    )


def rms_scale(values):
    return lax.rsqrt(jnp.mean(values * values, axis=-1, keepdims=True) + 1e-05)


def silu_slope(values):
    sigma = jax.nn.sigmoid(values)
    return sigma * (1.0 + values * (1.0 - sigma))


def embed(moment, width):
    half = width // 2
    freq = jnp.exp(-math.log(10000.0) * jnp.arange(half, dtype=jnp.float32) / half)
    angle = moment[:, None] * freq[None, :]
    return jnp.concatenate([jnp.sin(angle), jnp.cos(angle)], axis=-1)


def down_forward(hidden, embedding, in_matrix, out_matrix):
    lifted = hidden.astype(jnp.float32) + embedding
    normed = lifted * rms_scale(lifted)
    inner = jnp.dot(normed.astype(jnp.bfloat16), in_matrix, preferred_element_type=jnp.float32)
    gated = jax.nn.silu(inner).astype(jnp.bfloat16)
    return (lifted + jnp.dot(gated, out_matrix, preferred_element_type=jnp.float32)).astype(
        jnp.bfloat16
    )


def down_backward(hidden, embedding, in_matrix, out_matrix, cotan):
    lifted = hidden.astype(jnp.float32) + embedding
    scale = rms_scale(lifted)
    normed = lifted * scale
    normed_b = normed.astype(jnp.bfloat16)
    inner = jnp.dot(normed_b, in_matrix, preferred_element_type=jnp.float32)
    gated = jax.nn.silu(inner).astype(jnp.bfloat16)
    grad_out = rows_product(gated, cotan)
    d_gated = times_transposed(cotan, out_matrix)
    d_inner = (d_gated * silu_slope(inner)).astype(jnp.bfloat16)
    grad_in = rows_product(normed_b, d_inner)
    d_normed = times_transposed(d_inner, in_matrix)
    d_lifted = cotan.astype(jnp.float32) + scale * (
        d_normed - normed * jnp.mean(d_normed * normed, axis=-1, keepdims=True)
    )
    return (d_lifted.astype(jnp.bfloat16), grad_in, grad_out)


def up_forward(below, side, mix_matrix, up_matrix):
    joined = jnp.concatenate([below, side], axis=-1)
    mixed = jnp.dot(joined, mix_matrix, preferred_element_type=jnp.float32)
    normed = mixed * rms_scale(mixed)
    active = jax.nn.silu(normed).astype(jnp.bfloat16)
    return (mixed + jnp.dot(active, up_matrix, preferred_element_type=jnp.float32)).astype(
        jnp.bfloat16
    )


def up_backward(below, side, mix_matrix, up_matrix, cotan):
    width = below.shape[-1]
    joined = jnp.concatenate([below, side], axis=-1)
    mixed = jnp.dot(joined, mix_matrix, preferred_element_type=jnp.float32)
    scale = rms_scale(mixed)
    normed = mixed * scale
    active = jax.nn.silu(normed).astype(jnp.bfloat16)
    grad_up = rows_product(active, cotan)
    d_active = times_transposed(cotan, up_matrix)
    d_normed = d_active * silu_slope(normed)
    d_mixed = (
        cotan.astype(jnp.float32)
        + scale * (d_normed - normed * jnp.mean(d_normed * normed, axis=-1, keepdims=True))
    ).astype(jnp.bfloat16)
    grad_mix = rows_product(joined, d_mixed)
    d_joined = times_transposed(d_mixed, mix_matrix)
    return (d_joined[:, :width].astype(jnp.bfloat16), d_joined[:, width:], grad_mix, grad_up)


def up_forward_saving(below, side, mix_matrix, up_matrix):
    joined = jnp.concatenate([below, side], axis=-1)
    mixed = jnp.dot(joined, mix_matrix, preferred_element_type=jnp.float32)
    scale = rms_scale(mixed)
    normed = mixed * scale
    active = jax.nn.silu(normed).astype(jnp.bfloat16)
    result = (mixed + jnp.dot(active, up_matrix, preferred_element_type=jnp.float32)).astype(
        jnp.bfloat16
    )
    return result, (joined, scale, normed, active)


def up_backward_saved(saved, mix_matrix, up_matrix, cotan):
    joined, scale, normed, active = saved
    width = joined.shape[-1] // 2
    grad_up = rows_product(active, cotan)
    d_active = times_transposed(cotan, up_matrix)
    d_normed = d_active * silu_slope(normed)
    d_mixed = (
        cotan.astype(jnp.float32)
        + scale * (d_normed - normed * jnp.mean(d_normed * normed, axis=-1, keepdims=True))
    ).astype(jnp.bfloat16)
    grad_mix = rows_product(joined, d_mixed)
    d_joined = times_transposed(d_mixed, mix_matrix)
    return (d_joined[:, :width].astype(jnp.bfloat16), d_joined[:, width:], grad_mix, grad_up)


def keep_all(valid, new, old):
    if old is None:
        return new
    return tuple(jnp.where(valid, a, b) for a, b in zip(new, old))


def reduce_replicas(parts, tail, tail_shapes):
    shapes = [part.shape for part in parts] + list(tail_shapes)
    total = sum(math.prod(shape) for shape in shapes)
    groups = math.prod(lax.axis_size(name) for name in DP)
    lanes = 128
    length = -(-total // (lanes * groups)) * groups
    flat = jnp.concatenate([part.reshape(-1) for part in parts] + [tail])
    flat = jnp.pad(flat, (0, length * lanes - total)).reshape(length, lanes)
    for name in SCATTER:
        flat = scatter_sum(flat, name)
    flat = flat.astype(jnp.bfloat16)
    for name in reversed(SCATTER):
        flat = gather_all(flat, name)
    flat = flat.astype(jnp.float32) * (1.0 / groups)
    flat = flat.reshape(-1)
    out, start = [], 0
    for shape in shapes:
        out.append(flat[start : start + math.prod(shape)].reshape(shape))
        start += math.prod(shape)
    return tuple(out)


def axis_count(name):
    return math.prod(lax.axis_size(part) for part in (name if isinstance(name, tuple) else (name,)))


def scatter_sum(flat, name):
    count = axis_count(name)
    blocks = flat.astype(jnp.bfloat16).reshape(count, flat.shape[0] // count, flat.shape[1])
    got = lax.all_to_all(blocks, name, 0, 0, tiled=False)
    return jnp.sum(got.astype(jnp.float32), axis=0)


def gather_all(flat, name):
    count = axis_count(name)
    blocks = jnp.broadcast_to(flat[None], (count,) + flat.shape)
    return lax.all_to_all(blocks, name, 0, 0, tiled=False).reshape(-1, flat.shape[1])


def dp_split(mesh):
    column = mesh.devices[:, 0]
    sizes = [len({int(device.coords[axis]) for device in column}) for axis in (1, 0, 2)]
    if math.prod(sizes) != column.size:
        raise ValueError("dp split")
    return tuple(sizes)


def swap_core(value):
    return lax.ppermute(value, "core", [(0, 1), (1, 0)])


def hop(value, source, target):
    return lax.ppermute(value, "zh", [(source, target)])


def keep(valid, new, old):
    return new if old is None else jnp.where(valid, new, old)


def local(latents, clip_of_row, timestep, w_in, w_out, w_mix, w_up, out_grad):
    stages = lax.axis_size("zh")
    stage = lax.axis_index("zh")
    core = lax.axis_index("core")
    first = core == 0
    width = latents.shape[1]
    rows = latents.shape[0] // lax.axis_size("core")

    def pair(weights):
        own = weights[0]
        other = swap_core(own)
        return (jnp.where(first, own, other), jnp.where(first, other, own))

    in_pair, out_pair = pair(w_in), pair(w_out)

    offset = core * rows
    match = clip_of_row[0][:, None] == jnp.arange(timestep.shape[1], dtype=jnp.int32)[None, :]
    moment = jnp.sum(jnp.where(match, timestep[0][None, :], 0), axis=1).astype(jnp.float32)
    moment = lax.dynamic_slice_in_dim(moment, offset, rows)
    embedding = embed(moment, width)
    source = lax.dynamic_slice_in_dim(latents, offset, rows)
    seed = lax.dynamic_slice_in_dim(out_grad, offset, rows)

    down_in = [None, None]
    skip = [None, None]
    hidden = source
    for tick in range(stages):
        if tick > 0:
            hidden = hop(hidden, tick - 1, tick)
        valid = stage == tick
        lower = hidden
        upper = down_forward(lower, embedding, in_pair[0], out_pair[0])
        hidden = down_forward(upper, embedding, in_pair[1], out_pair[1])
        down_in = [keep(valid, lower, down_in[0]), keep(valid, upper, down_in[1])]
        skip = [keep(valid, upper, skip[0]), keep(valid, hidden, skip[1])]
        if tick == 0:
            w_mix, w_up, hidden = lax.optimization_barrier((w_mix, w_up, hidden))
            mix_pair, up_pair = pair(w_mix), pair(w_up)

    up_saved = [None, None]
    below = skip[1]
    for tick in range(stages):
        owner = stages - 1 - tick
        if tick > 0:
            below = hop(below, owner + 1, owner)
        valid = stage == owner
        middle, saved1 = up_forward_saving(below, skip[1], mix_pair[1], up_pair[1])
        below, saved0 = up_forward_saving(middle, skip[0], mix_pair[0], up_pair[0])
        up_saved = [keep_all(valid, saved0, up_saved[0]), keep_all(valid, saved1, up_saved[1])]

    d_skip = [None, None]
    grad_mix = [None, None]
    grad_up = [None, None]
    cotan = seed
    for tick in range(stages):
        if tick > 0:
            cotan = hop(cotan, tick - 1, tick)
        valid = stage == tick
        middle, side0, mix0, up0 = up_backward_saved(up_saved[0], mix_pair[0], up_pair[0], cotan)
        cotan, side1, mix1, up1 = up_backward_saved(up_saved[1], mix_pair[1], up_pair[1], middle)
        d_skip = [keep(valid, side0, d_skip[0]), keep(valid, side1, d_skip[1])]
        grad_mix = [keep(valid, mix0, grad_mix[0]), keep(valid, mix1, grad_mix[1])]
        grad_up = [keep(valid, up0, grad_up[0]), keep(valid, up1, grad_up[1])]

    def combine(grads):
        mine = jnp.where(first, grads[0], grads[1])
        theirs = jnp.where(first, grads[1], grads[0])
        return mine + swap_core(theirs.astype(jnp.bfloat16)).astype(jnp.float32)


    up_flat = jnp.concatenate(
        [combine(grad_mix).reshape(-1), combine(grad_up).reshape(-1)]
    )
    grad_in = [None, None]
    grad_out = [None, None]
    carry = cotan
    for tick in range(stages):
        owner = stages - 1 - tick
        if tick > 0:
            carry = hop(carry, owner + 1, owner)
        if tick == 1:
            carry, up_flat = lax.optimization_barrier((carry, up_flat))
        valid = stage == owner
        upper_c = (d_skip[1] + carry.astype(jnp.float32)).astype(jnp.bfloat16)
        upper_d, in1, out1 = down_backward(down_in[1], embedding, in_pair[1], out_pair[1], upper_c)
        lower_c = (d_skip[0] + upper_d.astype(jnp.float32)).astype(jnp.bfloat16)
        carry, in0, out0 = down_backward(down_in[0], embedding, in_pair[0], out_pair[0], lower_c)
        grad_in = [keep(valid, in0, grad_in[0]), keep(valid, in1, grad_in[1])]
        grad_out = [keep(valid, out0, grad_out[0]), keep(valid, out1, grad_out[1])]

    total_in, total_out, total_mix, total_up = reduce_replicas(
        (combine(grad_in), combine(grad_out)), up_flat, (grad_mix[0].shape, grad_up[0].shape)
    )
    return (total_in[None], total_out[None], total_mix[None], total_up[None])


def solution(mesh):
    sizes = dp_split(mesh)
    pipe = mesh.devices.shape[1]
    split = Mesh(mesh.devices.reshape(*sizes, pipe // 2, 2), DP + ("zh", "core"))
    sections = ("zh", "core")
    return jax.shard_map(
        local,
        mesh=split,
        in_specs=(
            P(DP, None),
            P(DP, None),
            P(DP, None),
            P(sections, None, None),
            P(sections, None, None),
            P(sections, None, None),
            P(sections, None, None),
            P(DP, None),
        ),
        out_specs=(
            P(sections, None, None),
            P(sections, None, None),
            P(sections, None, None),
            P(sections, None, None),
        ),
        check_vma=False,
    )
```
